128 devices in a mesh: dp: 32 (over y, x, core), tensor: 4 (over z).
Axes of the slice: x: 4, y: 4, z: 4, core: 2. Of those that a mesh axis runs over, the one named last changes fastest.
Arguments:
- layer_input: bfloat16 [4096, 2560], P('dp'), may hold values from -6 to 6
- inner_out: bfloat16 [4096, 2560], P('dp', 'tensor'), may hold values from -6 to 6
- out_grad: bfloat16 [4096, 2560], P('dp'), may hold values from -0.09375 to 0.09375
- zx_grad: bfloat16 [4096, 5120], P('dp', 'tensor'), may hold values from -0.09375 to 0.09375
- bc_grad: bfloat16 [4096, 1024], P('dp', 'tensor'), may hold values from -0.09375 to 0.09375
- dt_grad: bfloat16 [4096, 40], P('dp', 'tensor'), may hold values from -0.09375 to 0.09375
- owner_deal: int32 [4, 31], P('tensor'), may hold values from 0 to 31, as said below
- head_momentum: float32 [4, 2368, 2560], P('tensor', 'dp'), may hold values from -6 to 6
- bc_momentum: float32 [2, 128, 2560], replicated, may hold values from -6 to 6
Outputs:
- head_update: bfloat16 [40, 3, 64, 2560], P('tensor')
- dt_update: bfloat16 [40, 2560], P('tensor')
- bc_update: bfloat16 [2, 128, 2560], replicated
- head_momentum_out: float32 [4, 2368, 2560], P('tensor', 'dp')
- bc_momentum_out: float32 [2, 128, 2560], replicated
The draws below stay inside these ranges and needn't reach their ends.
Inputs may be any that keep to these rules, and one draw needn't show every extreme that they name: `owner_deal`: each owner holds at most 1 head blocks of one tensor index; the owner of the dt block (the last entry) holds exactly 1 head blocks of that index as well, so it holds exactly 74 rows.
All inputs are finite; a program needn't handle non-finite values.
Results may differ from the reference program's by a relative error of at most 0.0085.
Values may be sent and summed in bfloat16 or wider, within the bound.
No kernel may reach another device: no remote copies, remote signals or barrier semaphores. Data moves between devices by JAX's collectives and lax.ppermute only.
A program may use at most 128 MiB of HBM per device.

```python
import math
import jax
import jax.numpy as jnp
import numpy as np
from jax import lax

D = 2560
HD = 64
STATE = 128
HEADS = 40
NS_ITERS = 5
TOK_DEV = 128
TOKENS = 4096
INNER = 2560
HEADS_DEV = 10
OWN = 1
CAP = 74
BC_COLS = 1024
N_DP = 32
N_TENSOR = 4


def deal_single(subkey):
    key_order, key_full, key_rest = jax.random.split(subkey, 3)
    head_blocks = 3 * HEADS_DEV
    order = jax.random.permutation(key_order, head_blocks)
    full_owner = jax.random.randint(key_full, (), 0, N_DP)
    rest_slots = jax.random.permutation(key_rest, (N_DP - 1) * OWN)
    ranks = jnp.arange(head_blocks)
    picked = rest_slots[jnp.clip(ranks - OWN, 0, (N_DP - 1) * OWN - 1)]
    other_owner = picked // OWN
    other_owner = other_owner + (other_owner >= full_owner).astype(other_owner.dtype)
    owner_by_rank = jnp.where(ranks < OWN, full_owner, other_owner)
    owner_by_block = owner_by_rank[jnp.argsort(order)]
    return jnp.concatenate([owner_by_block.astype(jnp.int32), full_owner.astype(jnp.int32)[None]])


def draw_owner_deal(key, part):
    subkeys = jax.random.split(jax.random.fold_in(key, 17), N_TENSOR)
    return jax.vmap(deal_single)(subkeys).astype(jnp.int32)


def level_of(own_key, extent, cuts, low, largest):
    def one(position, parts):
        steps = jax.random.uniform(jax.random.fold_in(jax.random.fold_in(own_key, 6), position), (parts,), jnp.float32, low / len(cuts), largest / len(cuts))
        return jnp.repeat(jnp.exp(steps), extent[position] // parts).reshape((-1,) + (1,) * (len(extent) - position - 1))

    gain = one(*cuts[0])
    for cut in cuts[1:]:
        gain = gain * one(*cut)
    return gain


def noise(rng, dims, deviation, reach, cuts=(), kind=jnp.bfloat16):
    drawn = deviation * jax.random.normal(rng, dims, jnp.float32)
    if cuts:
        drawn = drawn * level_of(rng, dims, cuts, -0.22, 0.18)
    return jnp.clip(drawn, -reach, reach).astype(kind)


def setup_inputs(seed: int = 0) -> dict:
    arg_keys = jax.random.split(jax.random.key(seed), 10)
    return {
        "layer_input": noise(arg_keys[0], (TOKENS, D), 1.0, 6.0, ((0, 32),)),
        "inner_out": noise(arg_keys[1], (TOKENS, INNER), 1.0, 6.0, ((0, 32), (1, 4))),
        "out_grad": noise(arg_keys[2], (TOKENS, D), TOKENS ** -0.5, 0.09375, ((0, 32),)),
        "zx_grad": noise(arg_keys[3], (TOKENS, 2 * INNER), TOKENS ** -0.5, 0.09375, ((0, 32), (1, 4))),
        "bc_grad": noise(arg_keys[4], (TOKENS, BC_COLS), TOKENS ** -0.5, 0.09375, ((0, 32), (1, 4))),
        "dt_grad": noise(arg_keys[5], (TOKENS, HEADS), TOKENS ** -0.5, 0.09375, ((0, 32), (1, 4))),
        "owner_deal": draw_owner_deal(jax.random.fold_in(arg_keys[9], 71), 0),
        "head_momentum": noise(arg_keys[7], (N_TENSOR, N_DP * CAP, D), 1.0, 6.0, ((0, 4), (1, 32)), jnp.float32),
        "bc_momentum": noise(arg_keys[8], (2, STATE, D), 1.0, 6.0, (), jnp.float32),
    }


quintic_first = 3.4445
quintic_second = -4.775
quintic_third = 2.0315
momentum_decay = 0.95
norm_epsilon = 1e-07

def orthogonalize(moment):
    highest = lax.Precision.HIGHEST
    norm_value = jnp.sqrt(lax.optimization_barrier(jnp.sum(moment * moment, axis=(1, 2), keepdims=True)))
    current = moment / (norm_value + norm_epsilon)
    for step in range(NS_ITERS):
        gram_matrix = jnp.einsum('bik,bjk->bij', current, current, precision=highest)
        polynomial = quintic_second * gram_matrix + quintic_third * jnp.einsum('bij,bjk->bik', gram_matrix, gram_matrix, precision=highest)
        current = quintic_first * current + jnp.einsum('bij,bjk->bik', polynomial, current, precision=highest)
    return current

def row_tables(heads_here, head_dim):
    block_of_row = np.concatenate([np.repeat(np.arange(3 * heads_here), head_dim), np.full(heads_here, 3 * heads_here)])
    within = np.concatenate([np.tile(np.arange(head_dim), 3 * heads_here), np.arange(heads_here)])
    return (block_of_row.astype(np.int32), within.astype(np.int32))

def slot_rows(owner_list, heads_here, head_dim, capacity):
    block_count = owner_list.shape[0]
    positions = jnp.arange(block_count, dtype=jnp.int32)
    block_sizes = jnp.where(positions < block_count - 1, head_dim, heads_here).astype(jnp.int32)
    same_owner = owner_list[:, None] == owner_list[None, :]
    earlier = positions[:, None] < positions[None, :]
    offsets = lax.optimization_barrier(jnp.sum(jnp.where(same_owner & earlier, block_sizes[:, None], 0), axis=0)).astype(jnp.int32)
    block_of_row, within = row_tables(heads_here, head_dim)
    block_ids = jnp.asarray(block_of_row)
    return (owner_list[block_ids] * capacity + offsets[block_ids] + jnp.asarray(within)).astype(jnp.int32)

def rounded_product(left, right):
    contract = (((0,), (0,)), ((), ()))
    product = lax.dot_general(left, right, contract, preferred_element_type=jnp.float32)
    return lax.optimization_barrier(product.astype(jnp.bfloat16)).astype(jnp.float32)

def reference(layer_input, inner_out, out_grad, zx_grad, bc_grad, dt_grad, owner_deal, head_momentum, bc_momentum):
    heads_here = HEADS // N_TENSOR
    pieces = (layer_input.reshape(N_DP, TOK_DEV, D), inner_out.reshape(N_DP, TOK_DEV, HEADS * HD), out_grad.reshape(N_DP, TOK_DEV, D), zx_grad.reshape(N_DP, TOK_DEV, 2 * HEADS * HD), bc_grad.reshape(N_DP, TOK_DEV, N_TENSOR, 2 * STATE), dt_grad.reshape(N_DP, TOK_DEV, HEADS))

    def accumulate(totals, piece):
        tokens_in, inner_here, out_here, zx_here, bc_here, dt_here = piece
        zx_total, out_total, dt_total, bc_total = totals
        zx_total = zx_total + rounded_product(zx_here, tokens_in)
        out_total = out_total + rounded_product(inner_here, out_here)
        dt_total = dt_total + rounded_product(dt_here, tokens_in)
        for tensor_index in range(N_TENSOR):
            bc_total = bc_total + rounded_product(bc_here[:, tensor_index], tokens_in)
        return ((zx_total, out_total, dt_total, bc_total), None)
    start = (jnp.zeros((2 * HEADS * HD, D), jnp.float32), jnp.zeros((HEADS * HD, D), jnp.float32), jnp.zeros((HEADS, D), jnp.float32), jnp.zeros((2 * STATE, D), jnp.float32))
    (zx_total, out_total, dt_total, bc_total), unused = lax.scan(accumulate, start, pieces)
    zx_heads = zx_total.reshape(HEADS, 2 * HD, D)
    out_heads = out_total.reshape(HEADS, HD, D)
    head_parts = []
    dt_parts = []
    moment_parts = []
    for tensor_index in range(N_TENSOR):
        first = tensor_index * heads_here
        head_rows = jnp.concatenate([zx_heads[first:first + heads_here], out_heads[first:first + heads_here]], axis=1).reshape(3 * heads_here * HD, D)
        stacked_rows = jnp.concatenate([head_rows, dt_total[first:first + heads_here]], axis=0)
        slots = slot_rows(owner_deal[tensor_index], heads_here, HD, CAP)
        slot_sum = jnp.zeros((N_DP * CAP, D), jnp.float32).at[slots].set(stacked_rows)
        moment = momentum_decay * head_momentum[tensor_index] + slot_sum
        block_moment = jnp.take(moment, slots, axis=0)
        head_direction = orthogonalize(block_moment[:3 * heads_here * HD].reshape(3 * heads_here, HD, D))
        dt_direction = orthogonalize(block_moment[3 * heads_here * HD:][None])[0]
        head_parts.append((head_direction * math.sqrt(D)).astype(jnp.bfloat16).reshape(heads_here, 3, HD, D))
        dt_parts.append((dt_direction * math.sqrt(D)).astype(jnp.bfloat16))
        moment_parts.append(moment)
    bc_moment = momentum_decay * bc_momentum + bc_total.reshape(2, STATE, D)
    bc_update = (orthogonalize(bc_moment) * math.sqrt(D)).astype(jnp.bfloat16)
    head_update = jnp.concatenate(head_parts, axis=0)
    dt_update = jnp.concatenate(dt_parts, axis=0)
    head_momentum_out = jnp.stack(moment_parts, axis=0)
    return (head_update, dt_update, bc_update, head_momentum_out, bc_moment)
```

```python
import math

import jax
import jax.numpy as jnp
from jax import lax
from jax.sharding import PartitionSpec as P

HD = 64
STATE = 128
NS_ITERS = 5

quintic_first = 3.4445
quintic_second = -4.775
quintic_third = 2.0315
momentum_decay = 0.95
norm_epsilon = 1e-07

HEAD_REDUCE = "all_to_all"


def orthogonalize(moment):
    highest = lax.Precision.HIGHEST
    norm_value = jnp.sqrt(jnp.sum(moment * moment, axis=(1, 2), keepdims=True))
    current = moment / (norm_value + norm_epsilon)
    for step in range(NS_ITERS):
        gram_matrix = jnp.einsum("bik,bjk->bij", current, current, precision=highest)
        polynomial = quintic_second * gram_matrix + quintic_third * jnp.einsum(
            "bij,bjk->bik", gram_matrix, gram_matrix, precision=highest
        )
        current = quintic_first * current + jnp.einsum(
            "bij,bjk->bik", polynomial, current, precision=highest
        )
    return current


def on_device(
    layer_input,
    inner_out,
    out_grad,
    zx_grad,
    bc_grad,
    dt_grad,
    owner_deal,
    head_momentum,
    bc_momentum,
):
    n_data = lax.axis_size("dp")
    tokens, width = layer_input.shape
    heads_here = dt_grad.shape[1]
    capacity = head_momentum.shape[1]
    n_blocks = 3 * heads_here
    contract = (((0,), (0,)), ((), ()))
    f32, bf16 = jnp.float32, jnp.bfloat16

    owners = owner_deal[0]
    head_owner = owners[:n_blocks]
    dt_owner = owners[n_blocks]
    slots = jnp.arange(n_data, dtype=jnp.int32)

    bc_cols = lax.psum(bc_grad.astype(f32), "tensor")
    bc_part = lax.dot_general(
        bc_cols,
        layer_input.astype(f32),
        contract,
        precision=lax.Precision.HIGHEST,
        preferred_element_type=f32,
    )
    bc_summed = lax.psum(bc_part, "dp")

    zx = zx_grad.reshape(tokens, heads_here, 2, HD)
    io = inner_out.reshape(tokens, heads_here, 1, HD)
    upper = jnp.concatenate([zx, jnp.zeros_like(io)], axis=2).reshape(tokens, n_blocks, HD)
    lower = jnp.concatenate([jnp.zeros_like(zx), io], axis=2).reshape(tokens, n_blocks, HD)
    grad_blocks = jnp.concatenate([upper, lower], axis=0)
    pick = (head_owner[None, :] == slots[:, None]).astype(bf16)
    owner_cols = jnp.einsum(
        "tbr,ob->tor", grad_blocks, pick, preferred_element_type=f32
    ).astype(bf16)
    dt_cols = jnp.concatenate([dt_grad, jnp.zeros_like(dt_grad)], axis=0)
    is_dt = (slots == dt_owner).astype(bf16)
    dt_owner_cols = dt_cols[:, None, :] * is_dt[None, :, None]
    send_cols = jnp.concatenate([owner_cols, dt_owner_cols], axis=2).reshape(
        2 * tokens, n_data * capacity
    )
    factors = jnp.concatenate([layer_input, out_grad], axis=0)
    send = lax.dot_general(send_cols, factors, contract, preferred_element_type=f32).astype(bf16)

    if HEAD_REDUCE == "all_to_all":
        received = lax.all_to_all(send, "dp", split_axis=0, concat_axis=0, tiled=True)
        owned_sum = jnp.sum(
            received.reshape(n_data, capacity, width).astype(f32), axis=0
        )
    else:
        owned_sum = lax.psum_scatter(send, "dp", scatter_dimension=0, tiled=True).astype(f32)

    moment = momentum_decay * head_momentum[0] + owned_sum
    head_direction = orthogonalize(moment[None, :HD])[0]
    dt_direction = orthogonalize(moment[None, HD:])[0]
    owned_update = (
        jnp.concatenate([head_direction, dt_direction], axis=0) * math.sqrt(width)
    ).astype(bf16)
    everything = lax.all_gather(owned_update, "dp", axis=0, tiled=False)
    head_update = jnp.take(everything[:, :HD], head_owner, axis=0, mode="clip").reshape(
        heads_here, 3, HD, width
    )
    dt_update = lax.dynamic_index_in_dim(everything, dt_owner, axis=0, keepdims=False)[HD:]

    bc_moment = momentum_decay * bc_momentum + bc_summed.reshape(2, STATE, width)
    bc_update = (orthogonalize(bc_moment) * math.sqrt(width)).astype(bf16)
    return (head_update, dt_update, bc_update, moment[None], bc_moment)


def solution(mesh):
    in_specs = (
        P("dp", None),
        P("dp", "tensor"),
        P("dp", None),
        P("dp", "tensor"),
        P("dp", "tensor"),
        P("dp", "tensor"),
        P("tensor", None),
        P("tensor", "dp", None),
        P(),
    )
    out_specs = (
        P("tensor", None, None, None),
        P("tensor", None),
        P(),
        P("tensor", "dp", None),
        P(),
    )
    return jax.shard_map(
        on_device, mesh=mesh, in_specs=in_specs, out_specs=out_specs, check_vma=False
    )
```

```python
import math

import jax
import jax.numpy as jnp
from jax import lax
from jax.sharding import PartitionSpec as P

HD = 64
STATE = 128
NS_ITERS = 5

quintic_first = 3.4445
quintic_second = -4.775
quintic_third = 2.0315
momentum_decay = 0.95
norm_epsilon = 1e-07

def orthogonalize(moment):
    highest = lax.Precision.HIGHEST
    norm_value = jnp.sqrt(jnp.sum(moment * moment, axis=(1, 2), keepdims=True))
    current = moment / (norm_value + norm_epsilon)
    for step in range(NS_ITERS):
        gram_matrix = jnp.einsum("bik,bjk->bij", current, current, precision=highest)
        polynomial = quintic_second * gram_matrix + quintic_third * jnp.einsum(
            "bij,bjk->bik", gram_matrix, gram_matrix, precision=highest
        )
        current = quintic_first * current + jnp.einsum(
            "bij,bjk->bik", polynomial, current, precision=highest
        )
    return current


def on_device(
    layer_input,
    inner_out,
    out_grad,
    zx_grad,
    bc_grad,
    dt_grad,
    owner_deal,
    head_momentum,
    bc_momentum,
):
    n_data = lax.axis_size("dp")
    tokens, width = layer_input.shape
    heads_here = dt_grad.shape[1]
    capacity = head_momentum.shape[1]
    n_blocks = 3 * heads_here
    contract = (((0,), (0,)), ((), ()))
    f32, bf16 = jnp.float32, jnp.bfloat16

    owners = owner_deal[0]
    head_owner = owners[:n_blocks]
    dt_owner = owners[n_blocks]
    slots = jnp.arange(n_data, dtype=jnp.int32)

    bc_cols = jnp.sum(lax.all_gather(bc_grad, "tensor", axis=0).astype(f32), axis=0)
    bc_part = lax.dot_general(
        bc_cols,
        layer_input.astype(f32),
        contract,
        precision=lax.Precision.HIGHEST,
        preferred_element_type=f32,
    )
    bc_summed = lax.psum(bc_part, "dp")

    zx = zx_grad.reshape(tokens, heads_here, 2, HD)
    io = inner_out.reshape(tokens, heads_here, 1, HD)
    upper = jnp.concatenate([zx, jnp.zeros_like(io)], axis=2).reshape(tokens, n_blocks, HD)
    lower = jnp.concatenate([jnp.zeros_like(zx), io], axis=2).reshape(tokens, n_blocks, HD)
    grad_blocks = jnp.concatenate([upper, lower], axis=0)
    pick = (head_owner[None, :] == slots[:, None]).astype(bf16)
    owner_cols = jnp.einsum(
        "tbr,ob->tor", grad_blocks, pick, preferred_element_type=f32
    ).astype(bf16)
    dt_cols = jnp.concatenate([dt_grad, jnp.zeros_like(dt_grad)], axis=0)
    is_dt = (slots == dt_owner).astype(bf16)
    dt_owner_cols = dt_cols[:, None, :] * is_dt[None, :, None]
    chunk = -(-capacity // 16) * 16
    pad_cols = jnp.zeros((2 * tokens, n_data, chunk - capacity), bf16)
    send_cols = jnp.concatenate([owner_cols, dt_owner_cols, pad_cols], axis=2).reshape(
        2 * tokens, n_data * chunk
    )
    factors = jnp.concatenate([layer_input, out_grad], axis=0)
    send = lax.dot_general(send_cols, factors, contract, preferred_element_type=f32).astype(bf16)
    owned_sum = lax.psum_scatter(send, "dp", scatter_dimension=0, tiled=True)[:capacity].astype(f32)

    moment = momentum_decay * head_momentum[0] + owned_sum
    head_direction = orthogonalize(moment[None, :HD])[0]
    dt_direction = orthogonalize(moment[None, HD:])[0]
    head_gathered = lax.all_gather(
        (head_direction * math.sqrt(width)).astype(bf16), "dp", axis=0, tiled=False
    )
    tail = jnp.concatenate([dt_direction, jnp.zeros((chunk - capacity, width), f32)], axis=0)
    tail_gathered = lax.all_gather((tail * math.sqrt(width)).astype(bf16), "dp", axis=0, tiled=False)
    head_update = jnp.take(head_gathered, head_owner, axis=0, mode="clip").reshape(
        heads_here, 3, HD, width
    )
    dt_update = lax.dynamic_slice(tail_gathered, (dt_owner, 0, 0), (1, heads_here, width))[0]

    bc_moment = momentum_decay * bc_momentum + bc_summed.reshape(2, STATE, width)
    bc_update = (orthogonalize(bc_moment) * math.sqrt(width)).astype(bf16)
    return (head_update, dt_update, bc_update, moment[None], bc_moment)


def solution(mesh):
    in_specs = (
        P("dp", None),
        P("dp", "tensor"),
        P("dp", None),
        P("dp", "tensor"),
        P("dp", "tensor"),
        P("dp", "tensor"),
        P("tensor", None),
        P("tensor", "dp", None),
        P(),
    )
    out_specs = (
        P("tensor", None, None, None),
        P("tensor", None),
        P(),
        P("tensor", "dp", None),
        P(),
    )
    return jax.shard_map(
        on_device, mesh=mesh, in_specs=in_specs, out_specs=out_specs, check_vma=False
    )
```

```python
import math

import jax
import jax.numpy as jnp
from jax import lax
from jax.experimental import pallas as pl
from jax.experimental.pallas import tpu as pltpu
from jax.sharding import PartitionSpec as P

HD = 64
STATE = 128
NS_ITERS = 5

quintic_first = 3.4445
quintic_second = -4.775
quintic_third = 2.0315
momentum_decay = 0.95
norm_epsilon = 1e-07

def orthogonalize(moment):
    highest = lax.Precision.HIGH
    norm_value = jnp.sqrt(jnp.sum(moment * moment, axis=(1, 2), keepdims=True))
    current = moment / (norm_value + norm_epsilon)
    for step in range(NS_ITERS):
        gram_matrix = jnp.einsum("bik,bjk->bij", current, current, precision=highest)
        polynomial = quintic_second * gram_matrix + quintic_third * jnp.einsum(
            "bij,bjk->bik", gram_matrix, gram_matrix, precision=highest
        )
        current = quintic_first * current + jnp.einsum(
            "bij,bjk->bik", polynomial, current, precision=highest
        )
    return current


def _gather_kernel(index_ref, source_ref, out_ref, sems):
    rows = out_ref.shape[1]
    copies = []
    for b in range(out_ref.shape[0]):
        copy = pltpu.make_async_copy(
            source_ref.at[index_ref[b], pl.ds(0, rows)], out_ref.at[b], sems.at[b]
        )
        copy.start()
        copies.append(copy)
    for copy in copies:
        copy.wait()


def gather_slabs(source, index, rows):
    count = index.shape[0]
    n, chunk, width = source.shape
    index = jnp.clip(index, 0, n - 1).astype(jnp.int32)
    return pl.pallas_call(
        _gather_kernel,
        grid_spec=pltpu.PrefetchScalarGridSpec(
            num_scalar_prefetch=1,
            grid=(),
            in_specs=[pl.BlockSpec(memory_space=pl.ANY)],
            out_specs=pl.BlockSpec(memory_space=pltpu.VMEM),
            scratch_shapes=[pltpu.SemaphoreType.DMA((count,))],
        ),
        out_shape=jax.ShapeDtypeStruct((count, rows, width), source.dtype),
        cost_estimate=pl.CostEstimate(
            flops=0, transcendentals=0, bytes_accessed=2 * count * rows * width * source.dtype.itemsize
        ),
    )(index, source)


def on_device(
    layer_input,
    inner_out,
    out_grad,
    zx_grad,
    bc_grad,
    dt_grad,
    owner_deal,
    head_momentum,
    bc_momentum,
):
    n_data = lax.axis_size("dp")
    tokens, width = layer_input.shape
    heads_here = dt_grad.shape[1]
    capacity = head_momentum.shape[1]
    n_blocks = 3 * heads_here
    contract = (((0,), (0,)), ((), ()))
    f32, bf16 = jnp.float32, jnp.bfloat16

    owners = owner_deal[0]
    head_owner = owners[:n_blocks]
    dt_owner = owners[n_blocks]
    slots = jnp.arange(n_data, dtype=jnp.int32)

    bc_cols = jnp.sum(lax.all_gather(bc_grad, "tensor", axis=0).astype(f32), axis=0)
    bc_total = bc_cols.shape[1]
    bc_rows = bc_total // n_data
    bc_part = lax.dot_general(
        bc_cols,
        layer_input.astype(f32),
        contract,
        precision=lax.Precision.HIGHEST,
        preferred_element_type=f32,
    ).astype(bf16)
    bc_pieces = lax.all_to_all(bc_part, "dp", split_axis=0, concat_axis=0, tiled=True)
    bc_sum_rows = jnp.sum(bc_pieces.reshape(n_data, bc_rows, width).astype(f32), axis=0)
    me = lax.axis_index("dp")
    bc_flat = bc_momentum.reshape(bc_total, width)
    bc_moment_rows = momentum_decay * lax.dynamic_slice_in_dim(
        bc_flat, me * bc_rows, bc_rows, axis=0
    ) + bc_sum_rows
    bc_copies = jnp.broadcast_to(bc_moment_rows[None], (n_data, bc_rows, width))
    bc_moment = lax.all_to_all(bc_copies, "dp", split_axis=0, concat_axis=0, tiled=True)
    bc_moment = bc_moment.reshape(2, STATE, width)
    scale = math.sqrt(width)
    bc_update = (orthogonalize(bc_moment) * scale).astype(bf16)

    zx = zx_grad.reshape(tokens, heads_here, 2, HD)
    io = inner_out.reshape(tokens, heads_here, 1, HD)
    upper = jnp.concatenate([zx, jnp.zeros_like(io)], axis=2).reshape(tokens, n_blocks, HD)
    lower = jnp.concatenate([jnp.zeros_like(zx), io], axis=2).reshape(tokens, n_blocks, HD)
    grad_blocks = jnp.concatenate([upper, lower], axis=0)
    pick = (head_owner[None, :] == slots[:, None]).astype(bf16)
    owner_cols = jnp.einsum(
        "tbr,ob->tor", grad_blocks, pick, preferred_element_type=f32
    ).astype(bf16)
    dt_cols = jnp.concatenate([dt_grad, jnp.zeros_like(dt_grad)], axis=0)
    is_dt = (slots == dt_owner).astype(bf16)
    dt_owner_cols = dt_cols[:, None, :] * is_dt[None, :, None]
    chunk = -(-capacity // 16) * 16
    pad_cols = jnp.zeros((2 * tokens, n_data, chunk - capacity), bf16)
    send_cols = jnp.concatenate([owner_cols, dt_owner_cols, pad_cols], axis=2).reshape(
        2 * tokens, n_data * chunk
    )
    factors = jnp.concatenate([layer_input, out_grad], axis=0)
    send = lax.dot_general(send_cols, factors, contract, preferred_element_type=f32).astype(bf16)
    owned = lax.psum_scatter(send, "dp", scatter_dimension=0, tiled=True).astype(f32)
    owned_sum = owned[:capacity]

    moment = momentum_decay * head_momentum[0] + owned_sum
    head_direction = orthogonalize(moment[None, :HD])[0]
    dt_direction = orthogonalize(moment[None, HD:])[0]
    owned_update = jnp.concatenate(
        [
            (head_direction * scale).astype(bf16),
            (dt_direction * scale).astype(bf16),
            jnp.zeros((chunk - capacity, width), bf16),
        ],
        axis=0,
    )
    everything = lax.all_gather(owned_update, "dp", axis=0, tiled=False)
    head_update = gather_slabs(everything, head_owner, HD).reshape(heads_here, 3, HD, width)
    dt_update = lax.dynamic_slice(everything, (dt_owner, HD, 0), (1, heads_here, width))[0]
    return (head_update, dt_update, bc_update, moment[None], bc_moment)


def solution(mesh):
    in_specs = (
        P("dp", None),
        P("dp", "tensor"),
        P("dp", None),
        P("dp", "tensor"),
        P("dp", "tensor"),
        P("dp", "tensor"),
        P("tensor", None),
        P("tensor", "dp", None),
        P(),
    )
    out_specs = (
        P("tensor", None, None, None),
        P("tensor", None),
        P(),
        P("tensor", "dp", None),
        P(),
    )
    return jax.shard_map(
        on_device, mesh=mesh, in_specs=in_specs, out_specs=out_specs, check_vma=False
    )
```

```python
import math

import jax
import jax.numpy as jnp
from jax import lax
from jax.experimental import pallas as pl
from jax.experimental.pallas import tpu as pltpu
from jax.sharding import PartitionSpec as P

HD = 64
STATE = 128
NS_ITERS = 5

quintic_first = 3.4445
quintic_second = -4.775
quintic_third = 2.0315
momentum_decay = 0.95
norm_epsilon = 1e-07

def orthogonalize(moment):
    highest = lax.Precision.HIGH
    norm_value = jnp.sqrt(jnp.sum(moment * moment, axis=(1, 2), keepdims=True))
    current = moment / (norm_value + norm_epsilon)
    for step in range(NS_ITERS):
        gram_matrix = jnp.einsum("bik,bjk->bij", current, current, precision=highest)
        polynomial = quintic_second * gram_matrix + quintic_third * jnp.einsum(
            "bij,bjk->bik", gram_matrix, gram_matrix, precision=highest
        )
        current = quintic_first * current + jnp.einsum(
            "bij,bjk->bik", polynomial, current, precision=highest
        )
    return current


def _gather_kernel(index_ref, source_ref, out_ref, sems):
    rows = out_ref.shape[1]
    copies = []
    for b in range(out_ref.shape[0]):
        copy = pltpu.make_async_copy(
            source_ref.at[index_ref[b], pl.ds(0, rows)], out_ref.at[b], sems.at[b]
        )
        copy.start()
        copies.append(copy)
    for copy in copies:
        copy.wait()


def gather_slabs(source, index, rows):
    count = index.shape[0]
    n, chunk, width = source.shape
    index = jnp.clip(index, 0, n - 1).astype(jnp.int32)
    return pl.pallas_call(
        _gather_kernel,
        grid_spec=pltpu.PrefetchScalarGridSpec(
            num_scalar_prefetch=1,
            grid=(),
            in_specs=[pl.BlockSpec(memory_space=pl.ANY)],
            out_specs=pl.BlockSpec(memory_space=pltpu.VMEM),
            scratch_shapes=[pltpu.SemaphoreType.DMA((count,))],
        ),
        out_shape=jax.ShapeDtypeStruct((count, rows, width), source.dtype),
        cost_estimate=pl.CostEstimate(
            flops=0, transcendentals=0, bytes_accessed=2 * count * rows * width * source.dtype.itemsize
        ),
    )(index, source)


def on_device(
    layer_input,
    inner_out,
    out_grad,
    zx_grad,
    bc_grad,
    dt_grad,
    owner_deal,
    head_momentum,
    bc_momentum,
):
    n_data = lax.axis_size("dp")
    tokens, width = layer_input.shape
    heads_here = dt_grad.shape[1]
    capacity = head_momentum.shape[1]
    n_blocks = 3 * heads_here
    contract = (((0,), (0,)), ((), ()))
    f32, bf16 = jnp.float32, jnp.bfloat16

    owners = owner_deal[0]
    head_owner = owners[:n_blocks]
    dt_owner = owners[n_blocks]
    slots = jnp.arange(n_data, dtype=jnp.int32)

    bc_cols = jnp.sum(lax.all_gather(bc_grad, "tensor", axis=0).astype(f32), axis=0)
    bc_total = bc_cols.shape[1]
    bc_rows = bc_total // n_data
    bc_part = lax.dot_general(
        bc_cols,
        layer_input.astype(f32),
        contract,
        precision=lax.Precision.HIGHEST,
        preferred_element_type=f32,
    ).astype(bf16)
    bc_pieces = lax.all_to_all(bc_part, "dp", split_axis=0, concat_axis=0, tiled=True)
    bc_sum_rows = jnp.sum(bc_pieces.reshape(n_data, bc_rows, width).astype(f32), axis=0)
    me = lax.axis_index("dp")
    bc_flat = bc_momentum.reshape(bc_total, width)
    bc_moment_rows = momentum_decay * lax.dynamic_slice_in_dim(
        bc_flat, me * bc_rows, bc_rows, axis=0
    ) + bc_sum_rows
    bc_copies = jnp.broadcast_to(bc_moment_rows[None], (n_data, bc_rows, width))
    bc_moment = lax.all_to_all(bc_copies, "dp", split_axis=0, concat_axis=0, tiled=True)
    bc_moment = bc_moment.reshape(2, STATE, width)
    scale = math.sqrt(width)
    bc_update = (orthogonalize(bc_moment) * scale).astype(bf16)

    zx = zx_grad.reshape(tokens, heads_here, 2, HD)
    io = inner_out.reshape(tokens, heads_here, 1, HD)
    upper = jnp.concatenate([zx, jnp.zeros_like(io)], axis=2).reshape(tokens, n_blocks, HD)
    lower = jnp.concatenate([jnp.zeros_like(zx), io], axis=2).reshape(tokens, n_blocks, HD)
    grad_blocks = jnp.concatenate([upper, lower], axis=0)
    pick = (head_owner[None, :] == slots[:, None]).astype(bf16)
    owner_cols = jnp.einsum(
        "tbr,ob->tor", grad_blocks, pick, preferred_element_type=f32
    ).astype(bf16)
    dt_cols = jnp.concatenate([dt_grad, jnp.zeros_like(dt_grad)], axis=0)
    is_dt = (slots == dt_owner).astype(bf16)
    dt_owner_cols = dt_cols[:, None, :] * is_dt[None, :, None]
    chunk = -(-capacity // 16) * 16
    pad_cols = jnp.zeros((2 * tokens, n_data, chunk - capacity), bf16)
    send_cols = jnp.concatenate([owner_cols, dt_owner_cols, pad_cols], axis=2).reshape(
        2 * tokens, n_data * chunk
    )
    factors = jnp.concatenate([layer_input, out_grad], axis=0)
    send = lax.dot_general(send_cols, factors, contract, preferred_element_type=f32).astype(bf16)
    owned = lax.psum_scatter(send, "dp", scatter_dimension=0, tiled=True)
    owned, bc_update = lax.optimization_barrier((owned, bc_update))
    owned_sum = owned[:capacity].astype(f32)

    moment = momentum_decay * head_momentum[0] + owned_sum
    head_direction = orthogonalize(moment[None, :HD])[0]
    dt_direction = orthogonalize(moment[None, HD:])[0]
    owned_update = jnp.concatenate(
        [
            (head_direction * scale).astype(bf16),
            (dt_direction * scale).astype(bf16),
            jnp.zeros((chunk - capacity, width), bf16),
        ],
        axis=0,
    )
    everything = lax.all_gather(owned_update, "dp", axis=0, tiled=False)
    head_update = gather_slabs(everything, head_owner, HD).reshape(heads_here, 3, HD, width)
    dt_update = lax.dynamic_slice(everything, (dt_owner, HD, 0), (1, heads_here, width))[0]
    return (head_update, dt_update, bc_update, moment[None], bc_moment)


def solution(mesh):
    in_specs = (
        P("dp", None),
        P("dp", "tensor"),
        P("dp", None),
        P("dp", "tensor"),
        P("dp", "tensor"),
        P("dp", "tensor"),
        P("tensor", None),
        P("tensor", "dp", None),
        P(),
    )
    out_specs = (
        P("tensor", None, None, None),
        P("tensor", None),
        P(),
        P("tensor", "dp", None),
        P(),
    )
    return jax.shard_map(
        on_device, mesh=mesh, in_specs=in_specs, out_specs=out_specs, check_vma=False
    )
```

```python
import math

import jax
import jax.numpy as jnp
from jax import lax
from jax.experimental import pallas as pl
from jax.experimental.pallas import tpu as pltpu
from jax.sharding import PartitionSpec as P

HD = 64
STATE = 128
NS_ITERS = 5

quintic_first = 3.4445
quintic_second = -4.775
quintic_third = 2.0315
momentum_decay = 0.95
norm_epsilon = 1e-07

def orthogonalize(moment):
    highest = lax.Precision.HIGH
    norm_value = jnp.sqrt(jnp.sum(moment * moment, axis=(1, 2), keepdims=True))
    current = moment / (norm_value + norm_epsilon)
    for step in range(NS_ITERS):
        gram_matrix = jnp.einsum("bik,bjk->bij", current, current, precision=highest)
        polynomial = quintic_second * gram_matrix + quintic_third * jnp.einsum(
            "bij,bjk->bik", gram_matrix, gram_matrix, precision=highest
        )
        current = quintic_first * current + jnp.einsum(
            "bij,bjk->bik", polynomial, current, precision=highest
        )
    return current


def _gather_kernel(index_ref, source_ref, out_ref, sems):
    rows = out_ref.shape[1]
    copies = []
    for b in range(out_ref.shape[0]):
        copy = pltpu.make_async_copy(
            source_ref.at[index_ref[b], pl.ds(0, rows)], out_ref.at[b], sems.at[b]
        )
        copy.start()
        copies.append(copy)
    for copy in copies:
        copy.wait()


def gather_slabs(source, index, rows):
    count = index.shape[0]
    n, chunk, width = source.shape
    index = jnp.clip(index, 0, n - 1).astype(jnp.int32)
    return pl.pallas_call(
        _gather_kernel,
        grid_spec=pltpu.PrefetchScalarGridSpec(
            num_scalar_prefetch=1,
            grid=(),
            in_specs=[pl.BlockSpec(memory_space=pl.ANY)],
            out_specs=pl.BlockSpec(memory_space=pltpu.VMEM),
            scratch_shapes=[pltpu.SemaphoreType.DMA((count,))],
        ),
        out_shape=jax.ShapeDtypeStruct((count, rows, width), source.dtype),
        cost_estimate=pl.CostEstimate(
            flops=0, transcendentals=0, bytes_accessed=2 * count * rows * width * source.dtype.itemsize
        ),
    )(index, source)


def on_device(
    layer_input,
    inner_out,
    out_grad,
    zx_grad,
    bc_grad,
    dt_grad,
    owner_deal,
    head_momentum,
    bc_momentum,
):
    n_data = lax.axis_size("dp")
    tokens, width = layer_input.shape
    heads_here = dt_grad.shape[1]
    capacity = head_momentum.shape[1]
    n_blocks = 3 * heads_here
    contract = (((0,), (0,)), ((), ()))
    f32, bf16 = jnp.float32, jnp.bfloat16

    owners = owner_deal[0]
    head_owner = owners[:n_blocks]
    dt_owner = owners[n_blocks]
    slots = jnp.arange(n_data, dtype=jnp.int32)

    bc_cols = jnp.sum(lax.all_gather(bc_grad, "tensor", axis=0).astype(f32), axis=0)
    bc_total = bc_cols.shape[1]
    n_tensor = lax.axis_size("tensor")
    plane = lax.axis_index("tensor")
    plane_rows = bc_total // n_tensor
    bc_rows = plane_rows // n_data
    plane_cols = lax.dynamic_slice_in_dim(bc_cols, plane * plane_rows, plane_rows, axis=1)
    bc_part = lax.dot_general(
        plane_cols,
        layer_input.astype(f32),
        contract,
        precision=lax.Precision.HIGHEST,
        preferred_element_type=f32,
    ).astype(bf16)
    bc_pieces = lax.all_to_all(bc_part, "dp", split_axis=0, concat_axis=0, tiled=True)
    bc_sum_rows = jnp.sum(bc_pieces.reshape(n_data, bc_rows, width).astype(f32), axis=0)
    me = lax.axis_index("dp")
    bc_flat = bc_momentum.reshape(bc_total, width)
    bc_moment_rows = momentum_decay * lax.dynamic_slice_in_dim(
        bc_flat, plane * plane_rows + me * bc_rows, bc_rows, axis=0
    ) + bc_sum_rows
    bc_copies = jnp.broadcast_to(bc_moment_rows[None], (n_data, bc_rows, width))
    plane_moment = lax.all_to_all(bc_copies, "dp", split_axis=0, concat_axis=0, tiled=True)
    plane_moment = plane_moment.reshape(plane_rows, width)
    plane_copies = jnp.broadcast_to(plane_moment[None], (n_tensor, plane_rows, width))
    bc_moment = lax.all_to_all(plane_copies, "tensor", split_axis=0, concat_axis=0, tiled=True)
    bc_moment = bc_moment.reshape(2, STATE, width)
    scale = math.sqrt(width)
    bc_update = (orthogonalize(bc_moment) * scale).astype(bf16)

    zx = zx_grad.reshape(tokens, heads_here, 2, HD)
    io = inner_out.reshape(tokens, heads_here, 1, HD)
    upper = jnp.concatenate([zx, jnp.zeros_like(io)], axis=2).reshape(tokens, n_blocks, HD)
    lower = jnp.concatenate([jnp.zeros_like(zx), io], axis=2).reshape(tokens, n_blocks, HD)
    grad_blocks = jnp.concatenate([upper, lower], axis=0)
    pick = (head_owner[None, :] == slots[:, None]).astype(bf16)
    owner_cols = jnp.einsum(
        "tbr,ob->tor", grad_blocks, pick, preferred_element_type=f32
    ).astype(bf16)
    dt_cols = jnp.concatenate([dt_grad, jnp.zeros_like(dt_grad)], axis=0)
    is_dt = (slots == dt_owner).astype(bf16)
    dt_owner_cols = dt_cols[:, None, :] * is_dt[None, :, None]
    chunk = -(-capacity // 16) * 16
    pad_cols = jnp.zeros((2 * tokens, n_data, chunk - capacity), bf16)
    send_cols = jnp.concatenate([owner_cols, dt_owner_cols, pad_cols], axis=2).reshape(
        2 * tokens, n_data * chunk
    )
    factors = jnp.concatenate([layer_input, out_grad], axis=0)
    send = lax.dot_general(send_cols, factors, contract, preferred_element_type=f32).astype(bf16)
    owned = lax.psum_scatter(send, "dp", scatter_dimension=0, tiled=True)
    owned, bc_update = lax.optimization_barrier((owned, bc_update))
    owned_sum = owned[:capacity].astype(f32)

    moment = momentum_decay * head_momentum[0] + owned_sum
    head_direction = orthogonalize(moment[None, :HD])[0]
    dt_direction = orthogonalize(moment[None, HD:])[0]
    owned_update = jnp.concatenate(
        [
            (head_direction * scale).astype(bf16),
            (dt_direction * scale).astype(bf16),
            jnp.zeros((chunk - capacity, width), bf16),
        ],
        axis=0,
    )
    everything = lax.all_gather(owned_update, "dp", axis=0, tiled=False)
    head_update = gather_slabs(everything, head_owner, HD).reshape(heads_here, 3, HD, width)
    dt_update = lax.dynamic_slice(everything, (dt_owner, HD, 0), (1, heads_here, width))[0]
    return (head_update, dt_update, bc_update, moment[None], bc_moment)


def solution(mesh):
    in_specs = (
        P("dp", None),
        P("dp", "tensor"),
        P("dp", None),
        P("dp", "tensor"),
        P("dp", "tensor"),
        P("dp", "tensor"),
        P("tensor", None),
        P("tensor", "dp", None),
        P(),
    )
    out_specs = (
        P("tensor", None, None, None),
        P("tensor", None),
        P(),
        P("tensor", "dp", None),
        P(),
    )
    return jax.shard_map(
        on_device, mesh=mesh, in_specs=in_specs, out_specs=out_specs, check_vma=False
    )
```

```python
import math

import jax
import jax.numpy as jnp
from jax import lax
from jax.experimental import pallas as pl
from jax.experimental.pallas import tpu as pltpu
from jax.sharding import PartitionSpec as P

HD = 64
STATE = 128
NS_ITERS = 5

quintic_first = 3.4445
quintic_second = -4.775
quintic_third = 2.0315
momentum_decay = 0.95
norm_epsilon = 1e-07

def orthogonalize(moment):
    highest = lax.Precision.HIGH
    norm_value = jnp.sqrt(jnp.sum(moment * moment, axis=(1, 2), keepdims=True))
    current = moment / (norm_value + norm_epsilon)
    for step in range(NS_ITERS):
        gram_matrix = jnp.einsum("bik,bjk->bij", current, current, precision=highest)
        polynomial = quintic_second * gram_matrix + quintic_third * jnp.einsum(
            "bij,bjk->bik", gram_matrix, gram_matrix, precision=highest
        )
        current = quintic_first * current + jnp.einsum(
            "bij,bjk->bik", polynomial, current, precision=highest
        )
    return current


def _gather_kernel(index_ref, source_ref, out_ref, sems):
    rows = out_ref.shape[1]
    copies = []
    for b in range(out_ref.shape[0]):
        copy = pltpu.make_async_copy(
            source_ref.at[index_ref[b], pl.ds(0, rows)], out_ref.at[b], sems.at[b]
        )
        copy.start()
        copies.append(copy)
    for copy in copies:
        copy.wait()


def gather_slabs(source, index, rows):
    count = index.shape[0]
    n, chunk, width = source.shape
    index = jnp.clip(index, 0, n - 1).astype(jnp.int32)
    return pl.pallas_call(
        _gather_kernel,
        grid_spec=pltpu.PrefetchScalarGridSpec(
            num_scalar_prefetch=1,
            grid=(),
            in_specs=[pl.BlockSpec(memory_space=pl.ANY)],
            out_specs=pl.BlockSpec(memory_space=pltpu.VMEM),
            scratch_shapes=[pltpu.SemaphoreType.DMA((count,))],
        ),
        out_shape=jax.ShapeDtypeStruct((count, rows, width), source.dtype),
        cost_estimate=pl.CostEstimate(
            flops=0, transcendentals=0, bytes_accessed=2 * count * rows * width * source.dtype.itemsize
        ),
    )(index, source)


def on_device(
    layer_input,
    inner_out,
    out_grad,
    zx_grad,
    bc_grad,
    dt_grad,
    owner_deal,
    head_momentum,
    bc_momentum,
):
    n_data = lax.axis_size("dp")
    tokens, width = layer_input.shape
    heads_here = dt_grad.shape[1]
    capacity = head_momentum.shape[1]
    n_blocks = 3 * heads_here
    contract = (((0,), (0,)), ((), ()))
    f32, bf16 = jnp.float32, jnp.bfloat16

    owners = owner_deal[0]
    head_owner = owners[:n_blocks]
    dt_owner = owners[n_blocks]
    slots = jnp.arange(n_data, dtype=jnp.int32)

    bc_cols = jnp.sum(lax.all_gather(bc_grad, "tensor", axis=0).astype(f32), axis=0)
    bc_total = bc_cols.shape[1]
    n_tensor = lax.axis_size("tensor")
    plane = lax.axis_index("tensor")
    plane_rows = bc_total // n_tensor
    bc_rows = plane_rows // n_data
    plane_cols = lax.dynamic_slice_in_dim(bc_cols, plane * plane_rows, plane_rows, axis=1)
    bc_part = lax.dot_general(
        plane_cols,
        layer_input.astype(f32),
        contract,
        precision=lax.Precision.HIGHEST,
        preferred_element_type=f32,
    ).astype(bf16)
    dt_part = lax.dot_general(dt_grad, layer_input, contract, preferred_element_type=f32).astype(bf16)
    outgoing = jnp.concatenate(
        [
            bc_part.reshape(n_data, bc_rows, width),
            jnp.broadcast_to(dt_part[None], (n_data, heads_here, width)),
        ],
        axis=1,
    )
    incoming = lax.all_to_all(outgoing, "dp", split_axis=0, concat_axis=0, tiled=True)
    incoming_sum = jnp.sum(incoming.astype(f32), axis=0)
    bc_sum_rows = incoming_sum[:bc_rows]
    dt_sum = incoming_sum[bc_rows:]
    me = lax.axis_index("dp")
    bc_copies = jnp.broadcast_to(bc_sum_rows.astype(bf16)[None], (n_data, bc_rows, width))
    plane_sum = lax.all_to_all(bc_copies, "dp", split_axis=0, concat_axis=0, tiled=True)
    plane_sum = plane_sum.reshape(plane_rows, width)
    plane_copies = jnp.broadcast_to(plane_sum[None], (n_tensor, plane_rows, width))
    bc_sum = lax.all_to_all(plane_copies, "tensor", split_axis=0, concat_axis=0, tiled=True)
    bc_moment = momentum_decay * bc_momentum + bc_sum.astype(f32).reshape(2, STATE, width)
    scale = math.sqrt(width)
    bc_update = (orthogonalize(bc_moment) * scale).astype(bf16)

    zx = zx_grad.reshape(tokens, heads_here, 2, HD)
    io = inner_out.reshape(tokens, heads_here, 1, HD)
    upper = jnp.concatenate([zx, jnp.zeros_like(io)], axis=2).reshape(tokens, n_blocks, HD)
    lower = jnp.concatenate([jnp.zeros_like(zx), io], axis=2).reshape(tokens, n_blocks, HD)
    grad_blocks = jnp.concatenate([upper, lower], axis=0)
    pick = (head_owner[None, :] == slots[:, None]).astype(bf16)
    send_cols = jnp.einsum(
        "tbr,ob->tor", grad_blocks, pick, preferred_element_type=f32
    ).astype(bf16).reshape(2 * tokens, n_data * HD)
    factors = jnp.concatenate([layer_input, out_grad], axis=0)
    send = lax.dot_general(send_cols, factors, contract, preferred_element_type=f32).astype(bf16)
    owned = lax.psum_scatter(send, "dp", scatter_dimension=0, tiled=True)
    owned, bc_update, dt_sum = lax.optimization_barrier((owned, bc_update, dt_sum))
    dt_rows = jnp.where(me == dt_owner, dt_sum, jnp.zeros_like(dt_sum))
    owned_sum = jnp.concatenate([owned.astype(f32), dt_rows], axis=0)

    moment = momentum_decay * head_momentum[0] + owned_sum
    head_direction = orthogonalize(moment[None, :HD])[0]
    dt_direction = orthogonalize(moment[None, HD:])[0]
    chunk = -(-capacity // 16) * 16
    owned_update = jnp.concatenate(
        [
            (head_direction * scale).astype(bf16),
            (dt_direction * scale).astype(bf16),
            jnp.zeros((chunk - capacity, width), bf16),
        ],
        axis=0,
    )
    everything = lax.all_gather(owned_update, "dp", axis=0, tiled=False)
    head_update = gather_slabs(everything, head_owner, HD).reshape(heads_here, 3, HD, width)
    dt_update = lax.dynamic_slice(everything, (dt_owner, HD, 0), (1, heads_here, width))[0]
    return (head_update, dt_update, bc_update, moment[None], bc_moment)


def solution(mesh):
    in_specs = (
        P("dp", None),
        P("dp", "tensor"),
        P("dp", None),
        P("dp", "tensor"),
        P("dp", "tensor"),
        P("dp", "tensor"),
        P("tensor", None),
        P("tensor", "dp", None),
        P(),
    )
    out_specs = (
        P("tensor", None, None, None),
        P("tensor", None),
        P(),
        P("tensor", "dp", None),
        P(),
    )
    return jax.shard_map(
        on_device, mesh=mesh, in_specs=in_specs, out_specs=out_specs, check_vma=False
    )
```

```python
import math

import jax
import jax.numpy as jnp
from jax import lax
from jax.experimental import pallas as pl
from jax.experimental.pallas import tpu as pltpu
from jax.sharding import PartitionSpec as P

HD = 64
STATE = 128
NS_ITERS = 5

quintic_first = 3.4445
quintic_second = -4.775
quintic_third = 2.0315
momentum_decay = 0.95
norm_epsilon = 1e-07

def orthogonalize(moment):
    highest = lax.Precision.HIGH
    norm_value = jnp.sqrt(jnp.sum(moment * moment, axis=(1, 2), keepdims=True))
    current = moment / (norm_value + norm_epsilon)
    for step in range(NS_ITERS):
        gram_matrix = jnp.einsum("bik,bjk->bij", current, current, precision=highest)
        polynomial = quintic_second * gram_matrix + quintic_third * jnp.einsum(
            "bij,bjk->bik", gram_matrix, gram_matrix, precision=highest
        )
        current = quintic_first * current + jnp.einsum(
            "bij,bjk->bik", polynomial, current, precision=highest
        )
    return current


def _gather_kernel(index_ref, source_ref, out_ref, tail_ref, sems):
    count, rows = out_ref.shape[0], out_ref.shape[1]
    tail_rows = tail_ref.shape[0]
    copies = []
    for b in range(count):
        copies.append(
            pltpu.make_async_copy(
                source_ref.at[index_ref[b], pl.ds(0, rows)], out_ref.at[b], sems.at[b]
            )
        )
    copies.append(
        pltpu.make_async_copy(
            source_ref.at[index_ref[count], pl.ds(rows, tail_rows)], tail_ref, sems.at[count]
        )
    )
    for copy in copies:
        copy.start()
    for copy in copies:
        copy.wait()


def gather_slabs(source, index, rows, tail_rows):
    count = index.shape[0] - 1
    n, chunk, width = source.shape
    index = jnp.clip(index, 0, n - 1).astype(jnp.int32)
    moved = (count * rows + tail_rows) * width * source.dtype.itemsize
    return pl.pallas_call(
        _gather_kernel,
        grid_spec=pltpu.PrefetchScalarGridSpec(
            num_scalar_prefetch=1,
            grid=(),
            in_specs=[pl.BlockSpec(memory_space=pl.ANY)],
            out_specs=[
                pl.BlockSpec(memory_space=pltpu.VMEM),
                pl.BlockSpec(memory_space=pltpu.VMEM),
            ],
            scratch_shapes=[pltpu.SemaphoreType.DMA((count + 1,))],
        ),
        out_shape=[
            jax.ShapeDtypeStruct((count, rows, width), source.dtype),
            jax.ShapeDtypeStruct((tail_rows, width), source.dtype),
        ],
        cost_estimate=pl.CostEstimate(flops=0, transcendentals=0, bytes_accessed=2 * moved),
    )(index, source)


def on_device(
    layer_input,
    inner_out,
    out_grad,
    zx_grad,
    bc_grad,
    dt_grad,
    owner_deal,
    head_momentum,
    bc_momentum,
):
    n_data = lax.axis_size("dp")
    tokens, width = layer_input.shape
    heads_here = dt_grad.shape[1]
    capacity = head_momentum.shape[1]
    n_blocks = 3 * heads_here
    contract = (((0,), (0,)), ((), ()))
    f32, bf16 = jnp.float32, jnp.bfloat16

    owners = owner_deal[0]
    head_owner = owners[:n_blocks]
    dt_owner = owners[n_blocks]
    slots = jnp.arange(n_data, dtype=jnp.int32)

    bc_cols = jnp.sum(lax.all_gather(bc_grad, "tensor", axis=0).astype(f32), axis=0)
    bc_total = bc_cols.shape[1]
    n_tensor = lax.axis_size("tensor")
    plane = lax.axis_index("tensor")
    plane_rows = bc_total // n_tensor
    bc_rows = plane_rows // n_data
    plane_cols = lax.dynamic_slice_in_dim(bc_cols, plane * plane_rows, plane_rows, axis=1)
    bc_part = lax.dot_general(
        plane_cols,
        layer_input.astype(f32),
        contract,
        precision=lax.Precision.HIGHEST,
        preferred_element_type=f32,
    ).astype(bf16)
    bc_pieces = lax.all_to_all(bc_part, "dp", split_axis=0, concat_axis=0, tiled=True)
    bc_sum_rows = jnp.sum(bc_pieces.reshape(n_data, bc_rows, width).astype(f32), axis=0)
    bc_copies = jnp.broadcast_to(bc_sum_rows[None], (n_data, bc_rows, width))
    plane_sum = lax.all_to_all(bc_copies, "dp", split_axis=0, concat_axis=0, tiled=True)
    plane_sum = plane_sum.reshape(plane_rows, width)
    plane_copies = jnp.broadcast_to(plane_sum[None], (n_tensor, plane_rows, width))
    bc_sum = lax.all_to_all(plane_copies, "tensor", split_axis=0, concat_axis=0, tiled=True)
    bc_moment = momentum_decay * bc_momentum + bc_sum.reshape(2, STATE, width)
    scale = math.sqrt(width)
    bc_update = (orthogonalize(bc_moment) * scale).astype(bf16)

    zx = zx_grad.reshape(tokens, heads_here, 2, HD)
    io = inner_out.reshape(tokens, heads_here, 1, HD)
    upper = jnp.concatenate([zx, jnp.zeros_like(io)], axis=2).reshape(tokens, n_blocks, HD)
    lower = jnp.concatenate([jnp.zeros_like(zx), io], axis=2).reshape(tokens, n_blocks, HD)
    grad_blocks = jnp.concatenate([upper, lower], axis=0)
    pick = (head_owner[None, :] == slots[:, None]).astype(bf16)
    owner_cols = jnp.einsum(
        "tbr,ob->tor", grad_blocks, pick, preferred_element_type=f32
    ).astype(bf16)
    dt_cols = jnp.concatenate([dt_grad, jnp.zeros_like(dt_grad)], axis=0)
    is_dt = (slots == dt_owner).astype(bf16)
    dt_owner_cols = dt_cols[:, None, :] * is_dt[None, :, None]
    chunk = -(-capacity // 16) * 16
    pad_cols = jnp.zeros((2 * tokens, n_data, chunk - capacity), bf16)
    send_cols = jnp.concatenate([owner_cols, dt_owner_cols, pad_cols], axis=2).reshape(
        2 * tokens, n_data * chunk
    )
    factors = jnp.concatenate([layer_input, out_grad], axis=0)
    send = lax.dot_general(send_cols, factors, contract, preferred_element_type=f32).astype(bf16)
    owned = lax.psum_scatter(send, "dp", scatter_dimension=0, tiled=True)
    owned, bc_update = lax.optimization_barrier((owned, bc_update))
    owned_sum = owned[:capacity].astype(f32)

    moment = momentum_decay * head_momentum[0] + owned_sum
    head_direction = orthogonalize(moment[None, :HD])[0]
    dt_direction = orthogonalize(moment[None, HD:])[0]
    owned_update = jnp.concatenate(
        [
            (head_direction * scale).astype(bf16),
            (dt_direction * scale).astype(bf16),
            jnp.zeros((chunk - capacity, width), bf16),
        ],
        axis=0,
    )
    everything = lax.all_gather(owned_update, "dp", axis=0, tiled=False)
    head_update, tail = gather_slabs(everything, owners, HD, chunk - HD)
    dt_update = tail[:heads_here]
    head_update = head_update.reshape(heads_here, 3, HD, width)
    return (head_update, dt_update, bc_update, moment[None], bc_moment)


def solution(mesh):
    in_specs = (
        P("dp", None),
        P("dp", "tensor"),
        P("dp", None),
        P("dp", "tensor"),
        P("dp", "tensor"),
        P("dp", "tensor"),
        P("tensor", None),
        P("tensor", "dp", None),
        P(),
    )
    out_specs = (
        P("tensor", None, None, None),
        P("tensor", None),
        P(),
        P("tensor", "dp", None),
        P(),
    )
    return jax.shard_map(
        on_device, mesh=mesh, in_specs=in_specs, out_specs=out_specs, check_vma=False
    )
```

```python
import math

import jax
import jax.numpy as jnp
from jax import lax
from jax.experimental import pallas as pl
from jax.experimental.pallas import tpu as pltpu
from jax.sharding import PartitionSpec as P

HD = 64
STATE = 128
NS_ITERS = 5

quintic_first = 3.4445
quintic_second = -4.775
quintic_third = 2.0315
momentum_decay = 0.95
norm_epsilon = 1e-07

def orthogonalize(moment):
    highest = lax.Precision.HIGH
    norm_value = jnp.sqrt(jnp.sum(moment * moment, axis=(1, 2), keepdims=True))
    current = moment / (norm_value + norm_epsilon)
    for step in range(NS_ITERS):
        gram_matrix = jnp.einsum("bik,bjk->bij", current, current, precision=highest)
        polynomial = quintic_second * gram_matrix + quintic_third * jnp.einsum(
            "bij,bjk->bik", gram_matrix, gram_matrix, precision=highest
        )
        current = quintic_first * current + jnp.einsum(
            "bij,bjk->bik", polynomial, current, precision=highest
        )
    return current


def _gather_kernel(index_ref, source_ref, out_ref, tail_ref, sems):
    count, rows = out_ref.shape[0], out_ref.shape[1]
    tail_rows = tail_ref.shape[0]
    copies = []
    for b in range(count):
        copies.append(
            pltpu.make_async_copy(
                source_ref.at[index_ref[b], pl.ds(0, rows)], out_ref.at[b], sems.at[b]
            )
        )
    copies.append(
        pltpu.make_async_copy(
            source_ref.at[index_ref[count], pl.ds(rows, tail_rows)], tail_ref, sems.at[count]
        )
    )
    for copy in copies:
        copy.start()
    for copy in copies:
        copy.wait()


def gather_slabs(source, index, rows, tail_rows):
    count = index.shape[0] - 1
    n, chunk, width = source.shape
    index = jnp.clip(index, 0, n - 1).astype(jnp.int32)
    moved = (count * rows + tail_rows) * width * source.dtype.itemsize
    return pl.pallas_call(
        _gather_kernel,
        grid_spec=pltpu.PrefetchScalarGridSpec(
            num_scalar_prefetch=1,
            grid=(),
            in_specs=[pl.BlockSpec(memory_space=pl.ANY)],
            out_specs=[
                pl.BlockSpec(memory_space=pl.ANY),
                pl.BlockSpec(memory_space=pl.ANY),
            ],
            scratch_shapes=[pltpu.SemaphoreType.DMA((count + 1,))],
        ),
        out_shape=[
            jax.ShapeDtypeStruct((count, rows, width), source.dtype),
            jax.ShapeDtypeStruct((tail_rows, width), source.dtype),
        ],
        cost_estimate=pl.CostEstimate(flops=0, transcendentals=0, bytes_accessed=2 * moved),
    )(index, source)


def on_device(
    layer_input,
    inner_out,
    out_grad,
    zx_grad,
    bc_grad,
    dt_grad,
    owner_deal,
    head_momentum,
    bc_momentum,
):
    n_data = lax.axis_size("dp")
    tokens, width = layer_input.shape
    heads_here = dt_grad.shape[1]
    capacity = head_momentum.shape[1]
    n_blocks = 3 * heads_here
    contract = (((0,), (0,)), ((), ()))
    f32, bf16 = jnp.float32, jnp.bfloat16

    owners = owner_deal[0]
    head_owner = owners[:n_blocks]
    dt_owner = owners[n_blocks]
    slots = jnp.arange(n_data, dtype=jnp.int32)

    bc_cols = jnp.sum(lax.all_gather(bc_grad, "tensor", axis=0).astype(f32), axis=0)
    bc_total = bc_cols.shape[1]
    n_tensor = lax.axis_size("tensor")
    plane = lax.axis_index("tensor")
    plane_rows = bc_total // n_tensor
    bc_rows = plane_rows // n_data
    plane_cols = lax.dynamic_slice_in_dim(bc_cols, plane * plane_rows, plane_rows, axis=1)
    bc_part = lax.dot_general(
        plane_cols,
        layer_input.astype(f32),
        contract,
        precision=lax.Precision.HIGHEST,
        preferred_element_type=f32,
    ).astype(bf16)
    bc_pieces = lax.all_to_all(bc_part, "dp", split_axis=0, concat_axis=0, tiled=True)
    bc_sum_rows = jnp.sum(bc_pieces.reshape(n_data, bc_rows, width).astype(f32), axis=0)
    bc_copies = jnp.broadcast_to(bc_sum_rows[None], (n_data, bc_rows, width))
    plane_sum = lax.all_to_all(bc_copies, "dp", split_axis=0, concat_axis=0, tiled=True)
    plane_sum = plane_sum.reshape(plane_rows, width)
    plane_copies = jnp.broadcast_to(plane_sum[None], (n_tensor, plane_rows, width))
    bc_sum = lax.all_to_all(plane_copies, "tensor", split_axis=0, concat_axis=0, tiled=True)
    bc_moment = momentum_decay * bc_momentum + bc_sum.reshape(2, STATE, width)
    scale = math.sqrt(width)
    bc_update = (orthogonalize(bc_moment) * scale).astype(bf16)

    zx = zx_grad.reshape(tokens, heads_here, 2, HD)
    io = inner_out.reshape(tokens, heads_here, 1, HD)
    upper = jnp.concatenate([zx, jnp.zeros_like(io)], axis=2).reshape(tokens, n_blocks, HD)
    lower = jnp.concatenate([jnp.zeros_like(zx), io], axis=2).reshape(tokens, n_blocks, HD)
    grad_blocks = jnp.concatenate([upper, lower], axis=0)
    pick = (head_owner[None, :] == slots[:, None]).astype(bf16)
    owner_cols = jnp.einsum(
        "tbr,ob->tor", grad_blocks, pick, preferred_element_type=f32
    ).astype(bf16)
    dt_cols = jnp.concatenate([dt_grad, jnp.zeros_like(dt_grad)], axis=0)
    is_dt = (slots == dt_owner).astype(bf16)
    dt_owner_cols = dt_cols[:, None, :] * is_dt[None, :, None]
    chunk = -(-capacity // 16) * 16
    pad_cols = jnp.zeros((2 * tokens, n_data, chunk - capacity), bf16)
    send_cols = jnp.concatenate([owner_cols, dt_owner_cols, pad_cols], axis=2).reshape(
        2 * tokens, n_data * chunk
    )
    factors = jnp.concatenate([layer_input, out_grad], axis=0)
    send = lax.dot_general(send_cols, factors, contract, preferred_element_type=f32).astype(bf16)
    owned = lax.psum_scatter(send, "dp", scatter_dimension=0, tiled=True)
    owned, bc_update = lax.optimization_barrier((owned, bc_update))
    owned_sum = owned[:capacity].astype(f32)

    moment = momentum_decay * head_momentum[0] + owned_sum
    head_direction = orthogonalize(moment[None, :HD])[0]
    dt_direction = orthogonalize(moment[None, HD:])[0]
    owned_update = jnp.concatenate(
        [
            (head_direction * scale).astype(bf16),
            (dt_direction * scale).astype(bf16),
            jnp.zeros((chunk - capacity, width), bf16),
        ],
        axis=0,
    )
    everything = lax.all_gather(owned_update, "dp", axis=0, tiled=False)
    head_update, tail = gather_slabs(everything, owners, HD, chunk - HD)
    dt_update = tail[:heads_here]
    head_update = head_update.reshape(heads_here, 3, HD, width)
    return (head_update, dt_update, bc_update, moment[None], bc_moment)


def solution(mesh):
    in_specs = (
        P("dp", None),
        P("dp", "tensor"),
        P("dp", None),
        P("dp", "tensor"),
        P("dp", "tensor"),
        P("dp", "tensor"),
        P("tensor", None),
        P("tensor", "dp", None),
        P(),
    )
    out_specs = (
        P("tensor", None, None, None),
        P("tensor", None),
        P(),
        P("tensor", "dp", None),
        P(),
    )
    return jax.shard_map(
        on_device, mesh=mesh, in_specs=in_specs, out_specs=out_specs, check_vma=False
    )
```

```python
import math

import jax
import jax.numpy as jnp
from jax import lax
from jax.experimental import pallas as pl
from jax.experimental.pallas import tpu as pltpu
from jax.sharding import PartitionSpec as P

HD = 64
STATE = 128
NS_ITERS = 5

quintic_first = 3.4445
quintic_second = -4.775
quintic_third = 2.0315
momentum_decay = 0.95
norm_epsilon = 1e-07

def orthogonalize(moment):
    highest = lax.Precision.HIGH
    norm_value = jnp.sqrt(jnp.sum(moment * moment, axis=(1, 2), keepdims=True))
    current = moment / (norm_value + norm_epsilon)
    for step in range(NS_ITERS):
        gram_matrix = jnp.einsum("bik,bjk->bij", current, current, precision=highest)
        polynomial = quintic_second * gram_matrix + quintic_third * jnp.einsum(
            "bij,bjk->bik", gram_matrix, gram_matrix, precision=highest
        )
        current = quintic_first * current + jnp.einsum(
            "bij,bjk->bik", polynomial, current, precision=highest
        )
    return current


def _gather_kernel(index_ref, source_ref, out_ref, tail_ref, sems):
    count, rows = out_ref.shape[0], out_ref.shape[1]
    tail_rows = tail_ref.shape[0]
    copies = []
    for b in range(count):
        copies.append(
            pltpu.make_async_copy(
                source_ref.at[index_ref[b], pl.ds(0, rows)], out_ref.at[b], sems.at[b]
            )
        )
    copies.append(
        pltpu.make_async_copy(
            source_ref.at[index_ref[count], pl.ds(rows, tail_rows)], tail_ref, sems.at[count]
        )
    )
    for copy in copies:
        copy.start()
    for copy in copies:
        copy.wait()


def gather_slabs(source, index, rows, tail_rows):
    count = index.shape[0] - 1
    n, chunk, width = source.shape
    index = jnp.clip(index, 0, n - 1).astype(jnp.int32)
    moved = (count * rows + tail_rows) * width * source.dtype.itemsize
    return pl.pallas_call(
        _gather_kernel,
        grid_spec=pltpu.PrefetchScalarGridSpec(
            num_scalar_prefetch=1,
            grid=(),
            in_specs=[pl.BlockSpec(memory_space=pl.ANY)],
            out_specs=[
                pl.BlockSpec(memory_space=pltpu.VMEM),
                pl.BlockSpec(memory_space=pltpu.VMEM),
            ],
            scratch_shapes=[pltpu.SemaphoreType.DMA((count + 1,))],
        ),
        out_shape=[
            jax.ShapeDtypeStruct((count, rows, width), source.dtype),
            jax.ShapeDtypeStruct((tail_rows, width), source.dtype),
        ],
        cost_estimate=pl.CostEstimate(flops=0, transcendentals=0, bytes_accessed=2 * moved),
    )(index, source)


def on_device(
    layer_input,
    inner_out,
    out_grad,
    zx_grad,
    bc_grad,
    dt_grad,
    owner_deal,
    head_momentum,
    bc_momentum,
):
    n_data = lax.axis_size("dp")
    tokens, width = layer_input.shape
    heads_here = dt_grad.shape[1]
    capacity = head_momentum.shape[1]
    n_blocks = 3 * heads_here
    contract = (((0,), (0,)), ((), ()))
    f32, bf16 = jnp.float32, jnp.bfloat16

    owners = owner_deal[0]
    head_owner = owners[:n_blocks]
    dt_owner = owners[n_blocks]
    slots = jnp.arange(n_data, dtype=jnp.int32)

    bc_cols = jnp.sum(lax.all_gather(bc_grad, "tensor", axis=0).astype(f32), axis=0)
    bc_total = bc_cols.shape[1]
    n_tensor = lax.axis_size("tensor")
    plane = lax.axis_index("tensor")
    plane_rows = bc_total // n_tensor
    bc_rows = plane_rows // n_data
    plane_cols = lax.dynamic_slice_in_dim(bc_cols, plane * plane_rows, plane_rows, axis=1)
    bc_part = lax.dot_general(
        plane_cols,
        layer_input.astype(f32),
        contract,
        precision=lax.Precision.HIGHEST,
        preferred_element_type=f32,
    ).astype(bf16)
    bc_pieces = lax.all_to_all(bc_part, "dp", split_axis=0, concat_axis=0, tiled=True)
    bc_sum_rows = jnp.sum(bc_pieces.reshape(n_data, bc_rows, width).astype(f32), axis=0)
    bc_copies = jnp.broadcast_to(bc_sum_rows[None], (n_data, bc_rows, width))
    plane_sum = lax.all_to_all(bc_copies, "dp", split_axis=0, concat_axis=0, tiled=True)
    plane_sum = plane_sum.reshape(plane_rows, width)
    plane_copies = jnp.broadcast_to(plane_sum[None], (n_tensor, plane_rows, width))
    bc_sum = lax.all_to_all(plane_copies, "tensor", split_axis=0, concat_axis=0, tiled=True)
    bc_moment = momentum_decay * bc_momentum + bc_sum.reshape(2, STATE, width)
    scale = math.sqrt(width)
    bc_update = (orthogonalize(bc_moment) * scale).astype(bf16)

    zx = zx_grad.reshape(tokens, heads_here, 2, HD)
    io = inner_out.reshape(tokens, heads_here, 1, HD)
    upper = jnp.concatenate([zx, jnp.zeros_like(io)], axis=2).reshape(tokens, n_blocks, HD)
    lower = jnp.concatenate([jnp.zeros_like(zx), io], axis=2).reshape(tokens, n_blocks, HD)
    grad_blocks = jnp.concatenate([upper, lower], axis=0)
    pick = (head_owner[None, :] == slots[:, None]).astype(bf16)
    owner_cols = jnp.einsum(
        "tbr,ob->tor", grad_blocks, pick, preferred_element_type=f32
    ).astype(bf16)
    dt_cols = jnp.concatenate([dt_grad, jnp.zeros_like(dt_grad)], axis=0)
    is_dt = (slots == dt_owner).astype(bf16)
    dt_owner_cols = dt_cols[:, None, :] * is_dt[None, :, None]
    chunk = -(-capacity // 16) * 16
    pad_cols = jnp.zeros((2 * tokens, n_data, chunk - capacity), bf16)
    send_cols = jnp.concatenate([owner_cols, dt_owner_cols, pad_cols], axis=2).reshape(
        2 * tokens, n_data * chunk
    )
    factors = jnp.concatenate([layer_input, out_grad], axis=0)
    send = lax.dot_general(send_cols, factors, contract, preferred_element_type=f32).astype(bf16)
    owned = lax.psum_scatter(send, "dp", scatter_dimension=0, tiled=True)
    owned, bc_update = lax.optimization_barrier((owned, bc_update))
    owned_sum = owned[:capacity].astype(f32)

    moment = momentum_decay * head_momentum[0] + owned_sum
    dt_padded = jnp.concatenate(
        [moment[HD:], jnp.zeros((2 * HD - capacity, width), f32)], axis=0
    )
    directions = orthogonalize(jnp.stack([moment[:HD], dt_padded]))
    head_direction = directions[0]
    dt_direction = directions[1, : capacity - HD]
    owned_update = jnp.concatenate(
        [
            (head_direction * scale).astype(bf16),
            (dt_direction * scale).astype(bf16),
            jnp.zeros((chunk - capacity, width), bf16),
        ],
        axis=0,
    )
    everything = lax.all_gather(owned_update, "dp", axis=0, tiled=False)
    head_update, tail = gather_slabs(everything, owners, HD, chunk - HD)
    dt_update = tail[:heads_here]
    head_update = head_update.reshape(heads_here, 3, HD, width)
    return (head_update, dt_update, bc_update, moment[None], bc_moment)


def solution(mesh):
    in_specs = (
        P("dp", None),
        P("dp", "tensor"),
        P("dp", None),
        P("dp", "tensor"),
        P("dp", "tensor"),
        P("dp", "tensor"),
        P("tensor", None),
        P("tensor", "dp", None),
        P(),
    )
    out_specs = (
        P("tensor", None, None, None),
        P("tensor", None),
        P(),
        P("tensor", "dp", None),
        P(),
    )
    return jax.shard_map(
        on_device, mesh=mesh, in_specs=in_specs, out_specs=out_specs, check_vma=False
    )
```

```python
import math

import jax
import jax.numpy as jnp
from jax import lax
from jax.experimental import pallas as pl
from jax.experimental.pallas import tpu as pltpu
from jax.sharding import PartitionSpec as P

HD = 64
STATE = 128
NS_ITERS = 5

quintic_first = 3.4445
quintic_second = -4.775
quintic_third = 2.0315
momentum_decay = 0.95
norm_epsilon = 1e-07

def orthogonalize(moment):
    highest = lax.Precision.HIGH
    norm_value = jnp.sqrt(jnp.sum(moment * moment, axis=(1, 2), keepdims=True))
    current = moment / (norm_value + norm_epsilon)
    for step in range(NS_ITERS):
        gram_matrix = jnp.einsum("bik,bjk->bij", current, current, precision=highest)
        polynomial = quintic_second * gram_matrix + quintic_third * jnp.einsum(
            "bij,bjk->bik", gram_matrix, gram_matrix, precision=highest
        )
        current = quintic_first * current + jnp.einsum(
            "bij,bjk->bik", polynomial, current, precision=highest
        )
    return current


def _gather_kernel(index_ref, source_ref, out_ref, tail_ref, slabs, tail_slab, in_sems, out_sems):
    count, rows = slabs.shape[0], slabs.shape[1]
    tail_rows = tail_slab.shape[0]
    inbound = [
        pltpu.make_async_copy(
            source_ref.at[index_ref[b], pl.ds(0, rows)], slabs.at[b], in_sems.at[b]
        )
        for b in range(count)
    ]
    inbound.append(
        pltpu.make_async_copy(
            source_ref.at[index_ref[count], pl.ds(rows, tail_rows)], tail_slab, in_sems.at[count]
        )
    )
    outbound = [
        pltpu.make_async_copy(slabs.at[b], out_ref.at[b], out_sems.at[b]) for b in range(count)
    ]
    outbound.append(pltpu.make_async_copy(tail_slab, tail_ref, out_sems.at[count]))
    for copy in inbound:
        copy.start()
    for copy_in, copy_out in zip(inbound, outbound):
        copy_in.wait()
        copy_out.start()
    for copy in outbound:
        copy.wait()


def gather_slabs(source, index, rows, tail_rows):
    count = index.shape[0] - 1
    n, chunk, width = source.shape
    index = jnp.clip(index, 0, n - 1).astype(jnp.int32)
    moved = (count * rows + tail_rows) * width * source.dtype.itemsize
    return pl.pallas_call(
        _gather_kernel,
        grid_spec=pltpu.PrefetchScalarGridSpec(
            num_scalar_prefetch=1,
            grid=(),
            in_specs=[pl.BlockSpec(memory_space=pl.ANY)],
            out_specs=[
                pl.BlockSpec(memory_space=pl.ANY),
                pl.BlockSpec(memory_space=pl.ANY),
            ],
            scratch_shapes=[
                pltpu.VMEM((count, rows, width), source.dtype),
                pltpu.VMEM((tail_rows, width), source.dtype),
                pltpu.SemaphoreType.DMA((count + 1,)),
                pltpu.SemaphoreType.DMA((count + 1,)),
            ],
        ),
        out_shape=[
            jax.ShapeDtypeStruct((count, rows, width), source.dtype),
            jax.ShapeDtypeStruct((tail_rows, width), source.dtype),
        ],
        cost_estimate=pl.CostEstimate(flops=0, transcendentals=0, bytes_accessed=2 * moved),
    )(index, source)


def on_device(
    layer_input,
    inner_out,
    out_grad,
    zx_grad,
    bc_grad,
    dt_grad,
    owner_deal,
    head_momentum,
    bc_momentum,
):
    n_data = lax.axis_size("dp")
    tokens, width = layer_input.shape
    heads_here = dt_grad.shape[1]
    capacity = head_momentum.shape[1]
    n_blocks = 3 * heads_here
    contract = (((0,), (0,)), ((), ()))
    f32, bf16 = jnp.float32, jnp.bfloat16

    owners = owner_deal[0]
    head_owner = owners[:n_blocks]
    dt_owner = owners[n_blocks]
    slots = jnp.arange(n_data, dtype=jnp.int32)

    bc_cols = jnp.sum(lax.all_gather(bc_grad, "tensor", axis=0).astype(f32), axis=0)
    bc_total = bc_cols.shape[1]
    n_tensor = lax.axis_size("tensor")
    plane = lax.axis_index("tensor")
    plane_rows = bc_total // n_tensor
    bc_rows = plane_rows // n_data
    plane_cols = lax.dynamic_slice_in_dim(bc_cols, plane * plane_rows, plane_rows, axis=1)
    bc_part = lax.dot_general(
        plane_cols,
        layer_input.astype(f32),
        contract,
        precision=lax.Precision.HIGHEST,
        preferred_element_type=f32,
    ).astype(bf16)
    bc_pieces = lax.all_to_all(bc_part, "dp", split_axis=0, concat_axis=0, tiled=True)
    bc_sum_rows = jnp.sum(bc_pieces.reshape(n_data, bc_rows, width).astype(f32), axis=0)
    bc_copies = jnp.broadcast_to(bc_sum_rows[None], (n_data, bc_rows, width))
    plane_sum = lax.all_to_all(bc_copies, "dp", split_axis=0, concat_axis=0, tiled=True)
    plane_sum = plane_sum.reshape(plane_rows, width)
    plane_copies = jnp.broadcast_to(plane_sum[None], (n_tensor, plane_rows, width))
    bc_sum = lax.all_to_all(plane_copies, "tensor", split_axis=0, concat_axis=0, tiled=True)
    bc_moment = momentum_decay * bc_momentum + bc_sum.reshape(2, STATE, width)
    scale = math.sqrt(width)
    bc_update = (orthogonalize(bc_moment) * scale).astype(bf16)

    zx = zx_grad.reshape(tokens, heads_here, 2, HD)
    io = inner_out.reshape(tokens, heads_here, 1, HD)
    upper = jnp.concatenate([zx, jnp.zeros_like(io)], axis=2).reshape(tokens, n_blocks, HD)
    lower = jnp.concatenate([jnp.zeros_like(zx), io], axis=2).reshape(tokens, n_blocks, HD)
    grad_blocks = jnp.concatenate([upper, lower], axis=0)
    pick = (head_owner[None, :] == slots[:, None]).astype(bf16)
    owner_cols = jnp.einsum(
        "tbr,ob->tor", grad_blocks, pick, preferred_element_type=f32
    ).astype(bf16)
    dt_cols = jnp.concatenate([dt_grad, jnp.zeros_like(dt_grad)], axis=0)
    is_dt = (slots == dt_owner).astype(bf16)
    dt_owner_cols = dt_cols[:, None, :] * is_dt[None, :, None]
    chunk = -(-capacity // 16) * 16
    pad_cols = jnp.zeros((2 * tokens, n_data, chunk - capacity), bf16)
    send_cols = jnp.concatenate([owner_cols, dt_owner_cols, pad_cols], axis=2).reshape(
        2 * tokens, n_data * chunk
    )
    factors = jnp.concatenate([layer_input, out_grad], axis=0)
    send = lax.dot_general(send_cols, factors, contract, preferred_element_type=f32).astype(bf16)
    owned = lax.psum_scatter(send, "dp", scatter_dimension=0, tiled=True)
    owned, bc_update = lax.optimization_barrier((owned, bc_update))
    owned_sum = owned[:capacity].astype(f32)

    moment = momentum_decay * head_momentum[0] + owned_sum
    dt_padded = jnp.concatenate(
        [moment[HD:], jnp.zeros((2 * HD - capacity, width), f32)], axis=0
    )
    directions = orthogonalize(jnp.stack([moment[:HD], dt_padded]))
    head_direction = directions[0]
    dt_direction = directions[1, : capacity - HD]
    owned_update = jnp.concatenate(
        [
            (head_direction * scale).astype(bf16),
            (dt_direction * scale).astype(bf16),
            jnp.zeros((chunk - capacity, width), bf16),
        ],
        axis=0,
    )
    everything = lax.all_gather(owned_update, "dp", axis=0, tiled=False)
    head_update, tail = gather_slabs(everything, owners, HD, chunk - HD)
    dt_update = tail[:heads_here]
    head_update = head_update.reshape(heads_here, 3, HD, width)
    return (head_update, dt_update, bc_update, moment[None], bc_moment)


def solution(mesh):
    in_specs = (
        P("dp", None),
        P("dp", "tensor"),
        P("dp", None),
        P("dp", "tensor"),
        P("dp", "tensor"),
        P("dp", "tensor"),
        P("tensor", None),
        P("tensor", "dp", None),
        P(),
    )
    out_specs = (
        P("tensor", None, None, None),
        P("tensor", None),
        P(),
        P("tensor", "dp", None),
        P(),
    )
    return jax.shard_map(
        on_device, mesh=mesh, in_specs=in_specs, out_specs=out_specs, check_vma=False
    )
```

```python
import math

import jax
import jax.numpy as jnp
from jax import lax
from jax.experimental import pallas as pl
from jax.experimental.pallas import tpu as pltpu
from jax.sharding import PartitionSpec as P

HD = 64
STATE = 128
NS_ITERS = 5

quintic_first = 3.4445
quintic_second = -4.775
quintic_third = 2.0315
momentum_decay = 0.95
norm_epsilon = 1e-07

def orthogonalize(moment):
    highest = lax.Precision.HIGH
    norm_value = jnp.sqrt(jnp.sum(moment * moment, axis=(1, 2), keepdims=True))
    current = moment / (norm_value + norm_epsilon)
    for step in range(NS_ITERS):
        gram_matrix = jnp.einsum("bik,bjk->bij", current, current, precision=highest)
        polynomial = quintic_second * gram_matrix + quintic_third * jnp.einsum(
            "bij,bjk->bik", gram_matrix, gram_matrix, precision=highest
        )
        current = quintic_first * current + jnp.einsum(
            "bij,bjk->bik", polynomial, current, precision=highest
        )
    return current


def _gather_kernel(index_ref, source_ref, out_ref, tail_ref, sems):
    count, rows = out_ref.shape[0], out_ref.shape[1]
    tail_rows = tail_ref.shape[0]
    copies = []
    for b in range(count):
        copies.append(
            pltpu.make_async_copy(
                source_ref.at[index_ref[b], pl.ds(0, rows)], out_ref.at[b], sems.at[b]
            )
        )
    copies.append(
        pltpu.make_async_copy(
            source_ref.at[index_ref[count], pl.ds(rows, tail_rows)], tail_ref, sems.at[count]
        )
    )
    for copy in copies:
        copy.start()
    for copy in copies:
        copy.wait()


def gather_slabs(source, index, rows, tail_rows):
    count = index.shape[0] - 1
    n, chunk, width = source.shape
    index = jnp.clip(index, 0, n - 1).astype(jnp.int32)
    moved = (count * rows + tail_rows) * width * source.dtype.itemsize
    return pl.pallas_call(
        _gather_kernel,
        grid_spec=pltpu.PrefetchScalarGridSpec(
            num_scalar_prefetch=1,
            grid=(),
            in_specs=[pl.BlockSpec(memory_space=pl.ANY)],
            out_specs=[
                pl.BlockSpec(memory_space=pltpu.VMEM),
                pl.BlockSpec(memory_space=pltpu.VMEM),
            ],
            scratch_shapes=[pltpu.SemaphoreType.DMA((count + 1,))],
        ),
        out_shape=[
            jax.ShapeDtypeStruct((count, rows, width), source.dtype),
            jax.ShapeDtypeStruct((tail_rows, width), source.dtype),
        ],
        cost_estimate=pl.CostEstimate(flops=0, transcendentals=0, bytes_accessed=2 * moved),
    )(index, source)


def on_device(
    layer_input,
    inner_out,
    out_grad,
    zx_grad,
    bc_grad,
    dt_grad,
    owner_deal,
    head_momentum,
    bc_momentum,
):
    n_data = lax.axis_size("dp")
    tokens, width = layer_input.shape
    heads_here = dt_grad.shape[1]
    capacity = head_momentum.shape[1]
    n_blocks = 3 * heads_here
    contract = (((0,), (0,)), ((), ()))
    f32, bf16 = jnp.float32, jnp.bfloat16

    owners = owner_deal[0]
    head_owner = owners[:n_blocks]
    dt_owner = owners[n_blocks]
    slots = jnp.arange(n_data, dtype=jnp.int32)

    bc_cols = jnp.sum(lax.all_gather(bc_grad, "tensor", axis=0).astype(f32), axis=0)
    bc_total = bc_cols.shape[1]
    n_tensor = lax.axis_size("tensor")
    plane = lax.axis_index("tensor")
    plane_rows = bc_total // n_tensor
    bc_rows = plane_rows // n_data
    plane_cols = lax.dynamic_slice_in_dim(bc_cols, plane * plane_rows, plane_rows, axis=1)
    bc_part = lax.dot_general(
        plane_cols,
        layer_input.astype(f32),
        contract,
        precision=lax.Precision.HIGHEST,
        preferred_element_type=f32,
    ).astype(bf16)
    bc_pieces = lax.all_to_all(bc_part, "dp", split_axis=0, concat_axis=0, tiled=True)
    bc_sum_rows = jnp.sum(bc_pieces.reshape(n_data, bc_rows, width).astype(f32), axis=0)
    bc_copies = jnp.broadcast_to(bc_sum_rows.astype(bf16)[None], (n_data, bc_rows, width))
    plane_sum = lax.all_to_all(bc_copies, "dp", split_axis=0, concat_axis=0, tiled=True)
    plane_sum = plane_sum.reshape(plane_rows, width)
    plane_copies = jnp.broadcast_to(plane_sum[None], (n_tensor, plane_rows, width))
    bc_sum = lax.all_to_all(plane_copies, "tensor", split_axis=0, concat_axis=0, tiled=True)
    bc_moment = momentum_decay * bc_momentum + bc_sum.astype(f32).reshape(2, STATE, width)
    scale = math.sqrt(width)
    bc_update = (orthogonalize(bc_moment) * scale).astype(bf16)

    zx = zx_grad.reshape(tokens, heads_here, 2, HD)
    io = inner_out.reshape(tokens, heads_here, 1, HD)
    upper = jnp.concatenate([zx, jnp.zeros_like(io)], axis=2).reshape(tokens, n_blocks, HD)
    lower = jnp.concatenate([jnp.zeros_like(zx), io], axis=2).reshape(tokens, n_blocks, HD)
    grad_blocks = jnp.concatenate([upper, lower], axis=0)
    pick = (head_owner[None, :] == slots[:, None]).astype(bf16)
    owner_cols = jnp.einsum(
        "tbr,ob->tor", grad_blocks, pick, preferred_element_type=f32
    ).astype(bf16)
    dt_cols = jnp.concatenate([dt_grad, jnp.zeros_like(dt_grad)], axis=0)
    is_dt = (slots == dt_owner).astype(bf16)
    dt_owner_cols = dt_cols[:, None, :] * is_dt[None, :, None]
    chunk = -(-capacity // 16) * 16
    pad_cols = jnp.zeros((2 * tokens, n_data, chunk - capacity), bf16)
    send_cols = jnp.concatenate([owner_cols, dt_owner_cols, pad_cols], axis=2).reshape(
        2 * tokens, n_data * chunk
    )
    factors = jnp.concatenate([layer_input, out_grad], axis=0)
    send = lax.dot_general(send_cols, factors, contract, preferred_element_type=f32).astype(bf16)
    owned = lax.psum_scatter(send, "dp", scatter_dimension=0, tiled=True)
    owned, bc_update = lax.optimization_barrier((owned, bc_update))
    owned_sum = owned[:capacity].astype(f32)

    moment = momentum_decay * head_momentum[0] + owned_sum
    dt_padded = jnp.concatenate(
        [moment[HD:], jnp.zeros((2 * HD - capacity, width), f32)], axis=0
    )
    directions = orthogonalize(jnp.stack([moment[:HD], dt_padded]))
    head_direction = directions[0]
    dt_direction = directions[1, : capacity - HD]
    owned_update = jnp.concatenate(
        [
            (head_direction * scale).astype(bf16),
            (dt_direction * scale).astype(bf16),
            jnp.zeros((chunk - capacity, width), bf16),
        ],
        axis=0,
    )
    everything = lax.all_gather(owned_update, "dp", axis=0, tiled=False)
    head_update, tail = gather_slabs(everything, owners, HD, chunk - HD)
    dt_update = tail[:heads_here]
    head_update = head_update.reshape(heads_here, 3, HD, width)
    return (head_update, dt_update, bc_update, moment[None], bc_moment)


def solution(mesh):
    in_specs = (
        P("dp", None),
        P("dp", "tensor"),
        P("dp", None),
        P("dp", "tensor"),
        P("dp", "tensor"),
        P("dp", "tensor"),
        P("tensor", None),
        P("tensor", "dp", None),
        P(),
    )
    out_specs = (
        P("tensor", None, None, None),
        P("tensor", None),
        P(),
        P("tensor", "dp", None),
        P(),
    )
    return jax.shard_map(
        on_device, mesh=mesh, in_specs=in_specs, out_specs=out_specs, check_vma=False
    )
```

```python
import math

import jax
import jax.numpy as jnp
from jax import lax
from jax.experimental import pallas as pl
from jax.experimental.pallas import tpu as pltpu
from jax.sharding import PartitionSpec as P

HD = 64
STATE = 128
NS_ITERS = 5

quintic_first = 3.4445
quintic_second = -4.775
quintic_third = 2.0315
momentum_decay = 0.95
norm_epsilon = 1e-07

def orthogonalize(moment):
    highest = lax.Precision.HIGH
    norm_value = jnp.sqrt(jnp.sum(moment * moment, axis=(1, 2), keepdims=True))
    current = moment / (norm_value + norm_epsilon)
    for step in range(NS_ITERS):
        gram_matrix = jnp.einsum("bik,bjk->bij", current, current, precision=highest)
        polynomial = quintic_second * gram_matrix + quintic_third * jnp.einsum(
            "bij,bjk->bik", gram_matrix, gram_matrix, precision=highest
        )
        current = quintic_first * current + jnp.einsum(
            "bij,bjk->bik", polynomial, current, precision=highest
        )
    return current


def _gather_kernel(index_ref, source_ref, out_ref, tail_ref, sems):
    count, rows = out_ref.shape[0], out_ref.shape[1]
    tail_rows = tail_ref.shape[0]
    copies = []
    for b in range(count):
        copies.append(
            pltpu.make_async_copy(
                source_ref.at[index_ref[b], pl.ds(0, rows)], out_ref.at[b], sems.at[b]
            )
        )
    copies.append(
        pltpu.make_async_copy(
            source_ref.at[index_ref[count], pl.ds(rows, tail_rows)], tail_ref, sems.at[count]
        )
    )
    for copy in copies:
        copy.start()
    for copy in copies:
        copy.wait()


def gather_slabs(source, index, rows, tail_rows):
    count = index.shape[0] - 1
    n, chunk, width = source.shape
    index = jnp.clip(index, 0, n - 1).astype(jnp.int32)
    moved = (count * rows + tail_rows) * width * source.dtype.itemsize
    return pl.pallas_call(
        _gather_kernel,
        grid_spec=pltpu.PrefetchScalarGridSpec(
            num_scalar_prefetch=1,
            grid=(),
            in_specs=[pl.BlockSpec(memory_space=pl.ANY)],
            out_specs=[
                pl.BlockSpec(memory_space=pltpu.VMEM),
                pl.BlockSpec(memory_space=pltpu.VMEM),
            ],
            scratch_shapes=[pltpu.SemaphoreType.DMA((count + 1,))],
        ),
        out_shape=[
            jax.ShapeDtypeStruct((count, rows, width), source.dtype),
            jax.ShapeDtypeStruct((tail_rows, width), source.dtype),
        ],
        cost_estimate=pl.CostEstimate(flops=0, transcendentals=0, bytes_accessed=2 * moved),
    )(index, source)


def on_device(
    layer_input,
    inner_out,
    out_grad,
    zx_grad,
    bc_grad,
    dt_grad,
    owner_deal,
    head_momentum,
    bc_momentum,
):
    n_data = lax.axis_size("dp")
    tokens, width = layer_input.shape
    heads_here = dt_grad.shape[1]
    capacity = head_momentum.shape[1]
    n_blocks = 3 * heads_here
    contract = (((0,), (0,)), ((), ()))
    f32, bf16 = jnp.float32, jnp.bfloat16

    owners = owner_deal[0]
    slots = jnp.arange(n_data, dtype=jnp.int32)
    owner_hot = (owners[None, :] == slots[:, None]).astype(jnp.bfloat16)

    bc_cols = jnp.sum(lax.all_gather(bc_grad, "tensor", axis=0).astype(f32), axis=0)
    bc_total = bc_cols.shape[1]
    n_tensor = lax.axis_size("tensor")
    plane = lax.axis_index("tensor")
    plane_rows = bc_total // n_tensor
    bc_rows = plane_rows // n_data
    plane_cols = lax.dynamic_slice_in_dim(bc_cols, plane * plane_rows, plane_rows, axis=1)
    bc_part = lax.dot_general(
        plane_cols,
        layer_input.astype(f32),
        contract,
        precision=lax.Precision.HIGHEST,
        preferred_element_type=f32,
    ).astype(bf16)
    bc_pieces = lax.all_to_all(bc_part, "dp", split_axis=0, concat_axis=0, tiled=True)
    bc_sum_rows = jnp.sum(bc_pieces.reshape(n_data, bc_rows, width).astype(f32), axis=0)
    bc_copies = jnp.broadcast_to(bc_sum_rows[None], (n_data, bc_rows, width))
    plane_sum = lax.all_to_all(bc_copies, "dp", split_axis=0, concat_axis=0, tiled=True)
    plane_sum = plane_sum.reshape(plane_rows, width)
    plane_copies = jnp.broadcast_to(plane_sum[None], (n_tensor, plane_rows, width))
    bc_sum = lax.all_to_all(plane_copies, "tensor", split_axis=0, concat_axis=0, tiled=True)
    bc_moment = momentum_decay * bc_momentum + bc_sum.reshape(2, STATE, width)
    scale = math.sqrt(width)
    bc_update = (orthogonalize(bc_moment) * scale).astype(bf16)

    zx = zx_grad.reshape(tokens, heads_here, 2, HD)
    io = inner_out.reshape(tokens, heads_here, 1, HD)
    upper = jnp.concatenate([zx, jnp.zeros_like(io)], axis=2).reshape(tokens, n_blocks, HD)
    lower = jnp.concatenate([jnp.zeros_like(zx), io], axis=2).reshape(tokens, n_blocks, HD)
    grad_blocks = jnp.concatenate([upper, lower], axis=0)
    pick = owner_hot[:, :n_blocks]
    owner_cols = jnp.einsum(
        "tbr,ob->tor", grad_blocks, pick, preferred_element_type=f32
    ).astype(bf16)
    dt_cols = jnp.concatenate([dt_grad, jnp.zeros_like(dt_grad)], axis=0)
    is_dt = owner_hot[:, n_blocks]
    dt_owner_cols = dt_cols[:, None, :] * is_dt[None, :, None]
    chunk = -(-capacity // 16) * 16
    pad_cols = jnp.zeros((2 * tokens, n_data, chunk - capacity), bf16)
    send_cols = jnp.concatenate([owner_cols, dt_owner_cols, pad_cols], axis=2).reshape(
        2 * tokens, n_data * chunk
    )
    factors = jnp.concatenate([layer_input, out_grad], axis=0)
    send = lax.dot_general(send_cols, factors, contract, preferred_element_type=f32).astype(bf16)
    owned = lax.psum_scatter(send, "dp", scatter_dimension=0, tiled=True)
    owned, bc_update = lax.optimization_barrier((owned, bc_update))
    owned_sum = owned[:capacity].astype(f32)

    moment = momentum_decay * head_momentum[0] + owned_sum
    dt_padded = jnp.concatenate(
        [moment[HD:], jnp.zeros((2 * HD - capacity, width), f32)], axis=0
    )
    directions = orthogonalize(jnp.stack([moment[:HD], dt_padded]))
    head_direction = directions[0]
    dt_direction = directions[1, : capacity - HD]
    owned_update = jnp.concatenate(
        [
            (head_direction * scale).astype(bf16),
            (dt_direction * scale).astype(bf16),
            jnp.zeros((chunk - capacity, width), bf16),
        ],
        axis=0,
    )
    everything = lax.all_gather(owned_update, "dp", axis=0, tiled=False)
    head_update, tail = gather_slabs(everything, owners, HD, chunk - HD)
    dt_update = tail[:heads_here]
    head_update = head_update.reshape(heads_here, 3, HD, width)
    return (head_update, dt_update, bc_update, moment[None], bc_moment)


def solution(mesh):
    in_specs = (
        P("dp", None),
        P("dp", "tensor"),
        P("dp", None),
        P("dp", "tensor"),
        P("dp", "tensor"),
        P("dp", "tensor"),
        P("tensor", None),
        P("tensor", "dp", None),
        P(),
    )
    out_specs = (
        P("tensor", None, None, None),
        P("tensor", None),
        P(),
        P("tensor", "dp", None),
        P(),
    )
    return jax.shard_map(
        on_device, mesh=mesh, in_specs=in_specs, out_specs=out_specs, check_vma=False
    )
```

```python
import math

import jax
import jax.numpy as jnp
from jax import lax
from jax.experimental import pallas as pl
from jax.experimental.pallas import tpu as pltpu
from jax.sharding import PartitionSpec as P

HD = 64
STATE = 128
NS_ITERS = 5

quintic_first = 3.4445
quintic_second = -4.775
quintic_third = 2.0315
momentum_decay = 0.95
norm_epsilon = 1e-07

def orthogonalize(moment):
    highest = lax.Precision.HIGH
    norm_value = jnp.sqrt(jnp.sum(moment * moment, axis=(1, 2), keepdims=True))
    current = moment / (norm_value + norm_epsilon)
    for step in range(NS_ITERS):
        gram_matrix = jnp.einsum("bik,bjk->bij", current, current, precision=highest)
        polynomial = quintic_second * gram_matrix + quintic_third * jnp.einsum(
            "bij,bjk->bik", gram_matrix, gram_matrix, precision=highest
        )
        current = quintic_first * current + jnp.einsum(
            "bij,bjk->bik", polynomial, current, precision=highest
        )
    return current


def _gather_kernel(index_ref, source_ref, out_ref, tail_ref, sems):
    count, rows = out_ref.shape[0], out_ref.shape[1]
    tail_rows = tail_ref.shape[0]
    copies = []
    for b in range(count):
        copies.append(
            pltpu.make_async_copy(
                source_ref.at[index_ref[b], pl.ds(0, rows)], out_ref.at[b], sems.at[b]
            )
        )
    copies.append(
        pltpu.make_async_copy(
            source_ref.at[index_ref[count], pl.ds(rows, tail_rows)], tail_ref, sems.at[count]
        )
    )
    for copy in copies:
        copy.start()
    for copy in copies:
        copy.wait()


def gather_slabs(source, index, rows, tail_rows):
    count = index.shape[0] - 1
    n, chunk, width = source.shape
    index = jnp.clip(index, 0, n - 1).astype(jnp.int32)
    moved = (count * rows + tail_rows) * width * source.dtype.itemsize
    return pl.pallas_call(
        _gather_kernel,
        grid_spec=pltpu.PrefetchScalarGridSpec(
            num_scalar_prefetch=1,
            grid=(),
            in_specs=[pl.BlockSpec(memory_space=pl.ANY)],
            out_specs=[
                pl.BlockSpec(memory_space=pltpu.VMEM),
                pl.BlockSpec(memory_space=pltpu.VMEM),
            ],
            scratch_shapes=[pltpu.SemaphoreType.DMA((count + 1,))],
        ),
        out_shape=[
            jax.ShapeDtypeStruct((count, rows, width), source.dtype),
            jax.ShapeDtypeStruct((tail_rows, width), source.dtype),
        ],
        cost_estimate=pl.CostEstimate(flops=0, transcendentals=0, bytes_accessed=2 * moved),
    )(index, source)


def on_device(
    layer_input,
    inner_out,
    out_grad,
    zx_grad,
    bc_grad,
    dt_grad,
    owner_deal,
    head_momentum,
    bc_momentum,
):
    n_data = lax.axis_size("dp")
    tokens, width = layer_input.shape
    heads_here = dt_grad.shape[1]
    capacity = head_momentum.shape[1]
    n_blocks = 3 * heads_here
    contract = (((0,), (0,)), ((), ()))
    f32, bf16 = jnp.float32, jnp.bfloat16

    owners = owner_deal[0]
    slots = jnp.arange(n_data, dtype=jnp.int32)
    owner_hot = (owners[None, :] == slots[:, None]).astype(jnp.bfloat16)

    bc_cols = jnp.sum(lax.all_gather(bc_grad, "tensor", axis=0).astype(f32), axis=0)
    bc_total = bc_cols.shape[1]
    n_tensor = lax.axis_size("tensor")
    plane = lax.axis_index("tensor")
    plane_rows = bc_total // n_tensor
    bc_rows = plane_rows // n_data
    plane_cols = lax.dynamic_slice_in_dim(bc_cols, plane * plane_rows, plane_rows, axis=1)
    bc_part = lax.dot_general(
        plane_cols,
        layer_input.astype(f32),
        contract,
        precision=lax.Precision.HIGHEST,
        preferred_element_type=f32,
    ).astype(bf16)
    bc_pieces = lax.all_to_all(bc_part, "dp", split_axis=0, concat_axis=0, tiled=True)
    bc_sum_rows = jnp.sum(bc_pieces.reshape(n_data, bc_rows, width).astype(f32), axis=0)
    bc_copies = jnp.broadcast_to(bc_sum_rows[None], (n_data, bc_rows, width))
    plane_sum = lax.all_to_all(bc_copies, "dp", split_axis=0, concat_axis=0, tiled=True)
    plane_sum = plane_sum.reshape(plane_rows, width)
    plane_copies = jnp.broadcast_to(plane_sum[None], (n_tensor, plane_rows, width))
    bc_sum = lax.all_to_all(plane_copies, "tensor", split_axis=0, concat_axis=0, tiled=True)
    bc_moment = momentum_decay * bc_momentum + bc_sum.reshape(2, STATE, width)
    scale = math.sqrt(width)
    bc_update = (orthogonalize(bc_moment) * scale).astype(bf16)

    by_kind = owner_hot[:, :n_blocks].reshape(n_data, heads_here, 3)
    zx_blocks = zx_grad.reshape(tokens, 2 * heads_here, HD)
    io_blocks = inner_out.reshape(tokens, heads_here, HD)
    owner_zx = jnp.einsum(
        "tbr,ob->tor", zx_blocks, by_kind[:, :, :2].reshape(n_data, 2 * heads_here),
        preferred_element_type=f32,
    )
    owner_io = jnp.einsum(
        "tbr,ob->tor", io_blocks, by_kind[:, :, 2], preferred_element_type=f32
    )
    owner_cols = jnp.concatenate([owner_zx, owner_io], axis=0).astype(bf16)
    dt_cols = jnp.concatenate([dt_grad, jnp.zeros_like(dt_grad)], axis=0)
    is_dt = owner_hot[:, n_blocks]
    dt_owner_cols = dt_cols[:, None, :] * is_dt[None, :, None]
    chunk = -(-capacity // 16) * 16
    pad_cols = jnp.zeros((2 * tokens, n_data, chunk - capacity), bf16)
    send_cols = jnp.concatenate([owner_cols, dt_owner_cols, pad_cols], axis=2).reshape(
        2 * tokens, n_data * chunk
    )
    factors = jnp.concatenate([layer_input, out_grad], axis=0)
    send = lax.dot_general(send_cols, factors, contract, preferred_element_type=f32).astype(bf16)
    owned = lax.psum_scatter(send, "dp", scatter_dimension=0, tiled=True)
    owned, bc_update = lax.optimization_barrier((owned, bc_update))
    owned_sum = owned[:capacity].astype(f32)

    moment = momentum_decay * head_momentum[0] + owned_sum
    dt_padded = jnp.concatenate(
        [moment[HD:], jnp.zeros((2 * HD - capacity, width), f32)], axis=0
    )
    directions = orthogonalize(jnp.stack([moment[:HD], dt_padded]))
    head_direction = directions[0]
    dt_direction = directions[1, : capacity - HD]
    owned_update = jnp.concatenate(
        [
            (head_direction * scale).astype(bf16),
            (dt_direction * scale).astype(bf16),
            jnp.zeros((chunk - capacity, width), bf16),
        ],
        axis=0,
    )
    everything = lax.all_gather(owned_update, "dp", axis=0, tiled=False)
    head_update, tail = gather_slabs(everything, owners, HD, chunk - HD)
    dt_update = tail[:heads_here]
    head_update = head_update.reshape(heads_here, 3, HD, width)
    return (head_update, dt_update, bc_update, moment[None], bc_moment)


def solution(mesh):
    in_specs = (
        P("dp", None),
        P("dp", "tensor"),
        P("dp", None),
        P("dp", "tensor"),
        P("dp", "tensor"),
        P("dp", "tensor"),
        P("tensor", None),
        P("tensor", "dp", None),
        P(),
    )
    out_specs = (
        P("tensor", None, None, None),
        P("tensor", None),
        P(),
        P("tensor", "dp", None),
        P(),
    )
    return jax.shard_map(
        on_device, mesh=mesh, in_specs=in_specs, out_specs=out_specs, check_vma=False
    )
```

```python
import math

import jax
import jax.numpy as jnp
from jax import lax
from jax.experimental import pallas as pl
from jax.experimental.pallas import tpu as pltpu
from jax.sharding import PartitionSpec as P

HD = 64
STATE = 128
NS_ITERS = 5

quintic_first = 3.4445
quintic_second = -4.775
quintic_third = 2.0315
momentum_decay = 0.95
norm_epsilon = 1e-07

def orthogonalize(moment):
    highest = lax.Precision.HIGH
    norm_value = jnp.sqrt(jnp.sum(moment * moment, axis=(1, 2), keepdims=True))
    current = moment / (norm_value + norm_epsilon)
    for step in range(NS_ITERS):
        gram_matrix = jnp.einsum("bik,bjk->bij", current, current, precision=highest)
        polynomial = quintic_second * gram_matrix + quintic_third * jnp.einsum(
            "bij,bjk->bik", gram_matrix, gram_matrix, precision=highest
        )
        current = quintic_first * current + jnp.einsum(
            "bij,bjk->bik", polynomial, current, precision=highest
        )
    return current


def _gather_kernel(index_ref, source_ref, out_ref, tail_ref, sems):
    count, rows = out_ref.shape[0], out_ref.shape[1]
    tail_rows = tail_ref.shape[0]
    copies = []
    for b in range(count):
        copies.append(
            pltpu.make_async_copy(
                source_ref.at[index_ref[b], pl.ds(0, rows)], out_ref.at[b], sems.at[b]
            )
        )
    copies.append(
        pltpu.make_async_copy(
            source_ref.at[index_ref[count], pl.ds(rows, tail_rows)], tail_ref, sems.at[count]
        )
    )
    for copy in copies:
        copy.start()
    for copy in copies:
        copy.wait()


def gather_slabs(source, index, rows, tail_rows):
    count = index.shape[0] - 1
    n, chunk, width = source.shape
    index = jnp.clip(index, 0, n - 1).astype(jnp.int32)
    moved = (count * rows + tail_rows) * width * source.dtype.itemsize
    return pl.pallas_call(
        _gather_kernel,
        grid_spec=pltpu.PrefetchScalarGridSpec(
            num_scalar_prefetch=1,
            grid=(),
            in_specs=[pl.BlockSpec(memory_space=pl.ANY)],
            out_specs=[
                pl.BlockSpec(memory_space=pltpu.VMEM),
                pl.BlockSpec(memory_space=pltpu.VMEM),
            ],
            scratch_shapes=[pltpu.SemaphoreType.DMA((count + 1,))],
        ),
        out_shape=[
            jax.ShapeDtypeStruct((count, rows, width), source.dtype),
            jax.ShapeDtypeStruct((tail_rows, width), source.dtype),
        ],
        cost_estimate=pl.CostEstimate(flops=0, transcendentals=0, bytes_accessed=2 * moved),
    )(index, source)


def on_device(
    layer_input,
    inner_out,
    out_grad,
    zx_grad,
    bc_grad,
    dt_grad,
    owner_deal,
    head_momentum,
    bc_momentum,
):
    n_data = lax.axis_size("dp")
    tokens, width = layer_input.shape
    heads_here = dt_grad.shape[1]
    capacity = head_momentum.shape[1]
    n_blocks = 3 * heads_here
    contract = (((0,), (0,)), ((), ()))
    f32, bf16 = jnp.float32, jnp.bfloat16

    owners = owner_deal[0]
    slots = jnp.arange(n_data, dtype=jnp.int32)
    owner_hot = (owners[None, :] == slots[:, None]).astype(jnp.bfloat16)

    bc_cols = jnp.sum(lax.all_gather(bc_grad, "tensor", axis=0).astype(f32), axis=0)
    bc_total = bc_cols.shape[1]
    n_tensor = lax.axis_size("tensor")
    plane = lax.axis_index("tensor")
    plane_rows = bc_total // n_tensor
    bc_rows = plane_rows // n_data
    plane_cols = lax.dynamic_slice_in_dim(bc_cols, plane * plane_rows, plane_rows, axis=1)
    bc_part = lax.dot_general(
        plane_cols,
        layer_input.astype(f32),
        contract,
        precision=lax.Precision.HIGHEST,
        preferred_element_type=f32,
    ).astype(bf16)
    bc_pieces = lax.all_to_all(bc_part, "dp", split_axis=0, concat_axis=0, tiled=True)
    bc_sum_rows = jnp.sum(bc_pieces.reshape(n_data, bc_rows, width).astype(f32), axis=0)
    bc_copies = jnp.broadcast_to(bc_sum_rows[None], (n_data, bc_rows, width))
    plane_sum = lax.all_to_all(bc_copies, "dp", split_axis=0, concat_axis=0, tiled=True)
    plane_sum = plane_sum.reshape(plane_rows, width)
    plane_copies = jnp.broadcast_to(plane_sum[None], (n_tensor, plane_rows, width))
    bc_sum = lax.all_to_all(plane_copies, "tensor", split_axis=0, concat_axis=0, tiled=True)
    bc_moment = momentum_decay * bc_momentum + bc_sum.reshape(2, STATE, width)
    scale = math.sqrt(width)
    bc_update = (orthogonalize(bc_moment) * scale).astype(bf16)

    zx = zx_grad.reshape(tokens, heads_here, 2, HD)
    io = inner_out.reshape(tokens, heads_here, 1, HD)
    upper = jnp.concatenate([zx, jnp.zeros_like(io)], axis=2).reshape(tokens, n_blocks, HD)
    lower = jnp.concatenate([jnp.zeros_like(zx), io], axis=2).reshape(tokens, n_blocks, HD)
    grad_blocks = jnp.concatenate([upper, lower], axis=0)
    chunk = -(-capacity // 16) * 16
    dt_cols = jnp.concatenate([dt_grad, jnp.zeros_like(dt_grad)], axis=0)
    all_blocks = jnp.concatenate(
        [
            jnp.pad(grad_blocks, ((0, 0), (0, 0), (0, chunk - HD))),
            jnp.pad(dt_cols, ((0, 0), (HD, chunk - capacity)))[:, None, :],
        ],
        axis=1,
    )
    send_cols = jnp.einsum(
        "tbr,ob->tor", all_blocks, owner_hot, preferred_element_type=f32
    ).astype(bf16).reshape(2 * tokens, n_data * chunk)
    factors = jnp.concatenate([layer_input, out_grad], axis=0)
    send = lax.dot_general(send_cols, factors, contract, preferred_element_type=f32).astype(bf16)
    owned = lax.psum_scatter(send, "dp", scatter_dimension=0, tiled=True)
    owned, bc_update = lax.optimization_barrier((owned, bc_update))
    owned_sum = owned[:capacity].astype(f32)

    moment = momentum_decay * head_momentum[0] + owned_sum
    dt_padded = jnp.concatenate(
        [moment[HD:], jnp.zeros((2 * HD - capacity, width), f32)], axis=0
    )
    directions = orthogonalize(jnp.stack([moment[:HD], dt_padded]))
    head_direction = directions[0]
    dt_direction = directions[1, : capacity - HD]
    owned_update = jnp.concatenate(
        [
            (head_direction * scale).astype(bf16),
            (dt_direction * scale).astype(bf16),
            jnp.zeros((chunk - capacity, width), bf16),
        ],
        axis=0,
    )
    everything = lax.all_gather(owned_update, "dp", axis=0, tiled=False)
    head_update, tail = gather_slabs(everything, owners, HD, chunk - HD)
    dt_update = tail[:heads_here]
    head_update = head_update.reshape(heads_here, 3, HD, width)
    return (head_update, dt_update, bc_update, moment[None], bc_moment)


def solution(mesh):
    in_specs = (
        P("dp", None),
        P("dp", "tensor"),
        P("dp", None),
        P("dp", "tensor"),
        P("dp", "tensor"),
        P("dp", "tensor"),
        P("tensor", None),
        P("tensor", "dp", None),
        P(),
    )
    out_specs = (
        P("tensor", None, None, None),
        P("tensor", None),
        P(),
        P("tensor", "dp", None),
        P(),
    )
    return jax.shard_map(
        on_device, mesh=mesh, in_specs=in_specs, out_specs=out_specs, check_vma=False
    )
```
